128 devices in a mesh: sky: 8 (over x, y_hi), epoch: 16 (over y_lo, z, core).
Axes of the slice: x: 4, y: 4 (y_hi: 2, y_lo: 2; y = y_hi * 2 + y_lo), z: 4, core: 2. Of those that a mesh axis runs over, the one named last changes fastest.
Arguments:
- psi: bfloat16 [16, 512, 4096], P('epoch', 'sky'), may hold values from -6 to 6
- phi: bfloat16 [16, 512, 4096], P('epoch', 'sky'), may hold values from 0.25 to 4
- row_shift: int32 [16, 64], P(None, 'epoch'), may hold values from -8 to 8, as said below
- col_shift: int32 [16, 64], P(None, 'epoch'), may hold values from -64 to 64, as said below
Outputs:
- psi_stack: float32 [64, 512, 4096], P('epoch', 'sky')
- phi_stack: float32 [64, 512, 4096], P('epoch', 'sky')
The draws below stay inside these ranges and needn't reach their ends.
Inputs may be any that keep to these rules, and one draw needn't show every extreme that they name: `row_shift`: both ends of the range are taken by some epoch and hypothesis. `col_shift`: both ends of the range are taken by some epoch and hypothesis.
All inputs are finite; a program needn't handle non-finite values.
Results may differ from the reference program's by a relative error of at most 0.0003.
Values may be sent and summed in bfloat16 or wider, within the bound.
No kernel may reach another device: no remote copies, remote signals or barrier semaphores. Data moves between devices by JAX's collectives and lax.ppermute only.
A program may use at most 192 MiB of HBM per device.

```python
import math
import jax
import jax.numpy as jnp
from jax import lax

COLS = 4096
DEPTH = 8
XMAX = 64
EPOCHS = 16
HYPS = 64
ROWS = 512


def offset_table(key, reach):
    key_values, key_places = jax.random.split(key)
    offsets = jax.random.randint(key_values, (EPOCHS * HYPS,), -reach, reach + 1).astype(jnp.int32)
    positions = jax.random.permutation(key_places, EPOCHS * HYPS)
    offsets = offsets.at[positions[0]].set(reach).at[positions[1]].set(-reach)
    return offsets.reshape(EPOCHS, HYPS)


def draw_row_shift(key, part):
    return offset_table(jax.random.fold_in(key, 11), DEPTH)


def draw_col_shift(key, part):
    return offset_table(jax.random.fold_in(key, 23), XMAX)


def shard_levels(key, dims, shards, smallest, high):
    def one(axis_at, parts):
        heights = jax.random.uniform(jax.random.fold_in(jax.random.fold_in(key, 6), axis_at), (parts,), jnp.float32, smallest / len(shards), high / len(shards))
        return jnp.repeat(jnp.exp(heights), dims[axis_at] // parts).reshape((-1,) + (1,) * (len(dims) - axis_at - 1))

    loudness = one(*shards[0])
    for cut in shards[1:]:
        loudness = loudness * one(*cut)
    return loudness


def noise(key, extent, scale, most, shards=(), kind=jnp.bfloat16):
    loudness = shard_levels(key, extent, shards, -0.22, 0.18) if shards else 1.0
    drawn = jax.random.normal(key, extent, jnp.float32) * scale * loudness
    return jnp.minimum(jnp.maximum(drawn, -most), most).astype(kind)


def setup_inputs(seed: int = 0) -> dict:
    key_of = jax.random.split(jax.random.key(seed), 5)
    return {
        "psi": noise(key_of[0], (EPOCHS, ROWS, COLS), 1.0, 6.0, ((0, 16), (1, 8))),
        "phi": jnp.clip(jnp.exp(math.log(4.0) - 2.7725887 * jax.random.uniform(key_of[1], (EPOCHS, ROWS, COLS), jnp.float32) ** shard_levels(key_of[1], (EPOCHS, ROWS, COLS), ((0, 16), (1, 8)), -0.2, 0.2)), 0.25, 4.0).astype(jnp.bfloat16),
        "row_shift": draw_row_shift(jax.random.fold_in(key_of[4], 71), 0),
        "col_shift": draw_col_shift(jax.random.fold_in(key_of[4], 71), 0),
    }


def reference(psi, phi, row_shift, col_shift):
    images = jnp.stack([psi, phi], 1)
    padded = jnp.pad(images, ((0, 0), (0, 0), (DEPTH, DEPTH), (XMAX, XMAX)))

    def stack_hypothesis(hyp_index):
        def add_epoch(epoch_index, running):
            epoch_frame = lax.dynamic_index_in_dim(padded, epoch_index, 0, keepdims=False)
            row_start = (DEPTH + row_shift[epoch_index, hyp_index]).astype(jnp.int32)
            col_start = (XMAX + col_shift[epoch_index, hyp_index]).astype(jnp.int32)
            shifted = lax.dynamic_slice(epoch_frame, (jnp.int32(0), row_start, col_start), (2, ROWS, COLS))
            return running + shifted.astype(jnp.float32)

        return lax.fori_loop(0, EPOCHS, add_epoch, jnp.zeros((2, ROWS, COLS), jnp.float32))

    stacks = lax.map(stack_hypothesis, jnp.arange(HYPS, dtype=jnp.int32))
    return stacks[:, 0], stacks[:, 1]
```

```python
import functools

import jax
import jax.numpy as jnp
from jax import lax
from jax.experimental import pallas as pl
from jax.experimental.pallas import tpu as pltpu
from jax.sharding import PartitionSpec as P

DEPTH = 8
XMAX = 64
LANES = 128
BLOCK_COLS = 512
CHUNK_ROWS = 32


def with_halo(cells, sides, width):
    for axis, dim in sides:
        count = lax.axis_size(axis)
        ends = count - 1
        head = lax.slice_in_dim(cells, 0, width, axis=dim)
        tail = lax.slice_in_dim(cells, cells.shape[dim] - width, cells.shape[dim], axis=dim)
        cells = jnp.concatenate(
            [
                lax.ppermute(tail, axis, [(i, (i + 1) % count) for i in range(ends)]),
                cells,
                lax.ppermute(head, axis, [((i + 1) % count, i) for i in range(ends)]),
            ],
            axis=dim,
        )
    return cells


def stack_kernel(rs_ref, cs_ref, mid_ref, left_ref, right_ref, psi_ref, phi_ref, slab_ref,
                 *, epochs, hyps, rows_in, rows_out, width, blocks):
    j = pl.program_id(0)
    pieces = width // LANES
    slab_rows = slab_ref.shape[1]
    has_left = j > 0
    has_right = j < blocks - 1
    row_vregs = CHUNK_ROWS // 8

    for img, out_ref in ((0, psi_ref), (1, phi_ref)):
        def convert(e, carry):
            slab_ref[e, 0:rows_in, LANES:LANES + width] = mid_ref[e, img].astype(jnp.float32)
            left = left_ref[e, img].astype(jnp.float32)
            slab_ref[e, 0:rows_in, 0:LANES] = jnp.where(has_left, left, 0.0)
            right = right_ref[e, img].astype(jnp.float32)
            slab_ref[e, 0:rows_in, LANES + width:2 * LANES + width] = jnp.where(has_right, right, 0.0)
            slab_ref[e, rows_in:slab_rows, :] = jnp.zeros((slab_rows - rows_in, width + 2 * LANES), jnp.float32)
            return carry

        lax.fori_loop(0, epochs, convert, 0)

        for h in range(hyps):
            for chunk in range(rows_out // CHUNK_ROWS):
                y0 = chunk * CHUNK_ROWS

                def add_epoch(e, acc):
                    start = DEPTH + rs_ref[e * hyps + h]
                    col = cs_ref[e * hyps + h]
                    a8 = start // 8
                    b8 = start - a8 * 8
                    q = (col + LANES) // LANES - 1
                    rem = col - q * LANES
                    row0 = pl.multiple_of(y0 + a8 * 8, 8)
                    lane0 = pl.multiple_of((q + 1) * LANES, LANES)
                    sub_mask = lax.broadcasted_iota(jnp.int32, (8, LANES), 0) >= b8
                    lane_mask = lax.broadcasted_iota(jnp.int32, (8, LANES), 1) >= rem
                    sub_shift = lax.rem(8 - b8, 8)
                    lane_shift = lax.rem(LANES - rem, LANES)
                    window = slab_ref.at[e, pl.ds(row0, CHUNK_ROWS + 8), pl.ds(lane0, width + LANES)]
                    tiles = [
                        [window[8 * k:8 * k + 8, LANES * p:LANES * p + LANES] for p in range(pieces + 1)]
                        for k in range(row_vregs + 1)
                    ]
                    out = []
                    for k in range(row_vregs):
                        shifted = [
                            pltpu.roll(jnp.where(sub_mask, tiles[k][p], tiles[k + 1][p]), sub_shift, 0)
                            for p in range(pieces + 1)
                        ]
                        out.append([
                            acc[k][p] + pltpu.roll(jnp.where(lane_mask, shifted[p], shifted[p + 1]), lane_shift, 1)
                            for p in range(pieces)
                        ])
                    return out

                zero = [[jnp.zeros((8, LANES), jnp.float32) for _ in range(pieces)] for _ in range(row_vregs)]
                acc = lax.fori_loop(0, epochs, add_epoch, zero, unroll=4)
                for k in range(row_vregs):
                    for p in range(pieces):
                        out_ref[h, pl.ds(y0 + 8 * k, 8), pl.ds(LANES * p, LANES)] = acc[k][p]


def stack_call(extended, rs, cs, hyps, rows_out):
    epochs, images, rows_in, cols = extended.shape
    width = BLOCK_COLS
    blocks = cols // width
    pieces = width // LANES
    last_piece = cols // LANES - 1
    kernel = functools.partial(
        stack_kernel, epochs=epochs, hyps=hyps, rows_in=rows_in, rows_out=rows_out, width=width, blocks=blocks
    )
    grid_spec = pltpu.PrefetchScalarGridSpec(
        num_scalar_prefetch=2,
        grid=(blocks,),
        in_specs=[
            pl.BlockSpec((epochs, images, rows_in, width), lambda j, rs, cs: (0, 0, 0, j)),
            pl.BlockSpec((epochs, images, rows_in, LANES),
                         lambda j, rs, cs: (0, 0, 0, jnp.maximum(j * pieces - 1, 0))),
            pl.BlockSpec((epochs, images, rows_in, LANES),
                         lambda j, rs, cs: (0, 0, 0, jnp.minimum((j + 1) * pieces, last_piece))),
        ],
        out_specs=[
            pl.BlockSpec((hyps, rows_out, width), lambda j, rs, cs: (0, 0, j)),
            pl.BlockSpec((hyps, rows_out, width), lambda j, rs, cs: (0, 0, j)),
        ],
        scratch_shapes=[pltpu.VMEM((epochs, rows_in + 8, width + 2 * LANES), jnp.float32)],
    )
    out_shape = [jax.ShapeDtypeStruct((hyps, rows_out, cols), jnp.float32)] * 2
    flops = 2 * epochs * hyps * images * rows_out * cols
    return pl.pallas_call(
        kernel,
        grid_spec=grid_spec,
        out_shape=out_shape,
        compiler_params=pltpu.CompilerParams(dimension_semantics=("arbitrary",)),
        cost_estimate=pl.CostEstimate(
            flops=flops, transcendentals=0, bytes_accessed=extended.size * 2 + 2 * hyps * rows_out * cols * 4
        ),
        name="shift_stack",
    )(rs, cs, extended, extended, extended)


def body(psi, phi, row_shift, col_shift):
    row_count = psi.shape[1]
    hyp_count = row_shift.shape[1]
    images = jnp.stack([psi, phi], 1)
    extended = with_halo(images, (("sky", 2),), DEPTH)
    gathered = lax.all_gather(extended, "epoch", axis=0, tiled=True)
    rs = row_shift.reshape(-1)
    cs = col_shift.reshape(-1)
    psi_out, phi_out = stack_call(gathered, rs, cs, hyp_count, row_count)
    return psi_out, phi_out


def solution(mesh):
    return jax.shard_map(
        body,
        mesh=mesh,
        in_specs=(
            P("epoch", "sky", None),
            P("epoch", "sky", None),
            P(None, "epoch"),
            P(None, "epoch"),
        ),
        out_specs=(P("epoch", "sky", None), P("epoch", "sky", None)),
        check_vma=False,
    )
```

```python
import functools

import jax
import jax.numpy as jnp
from jax import lax
from jax.experimental import pallas as pl
from jax.experimental.pallas import tpu as pltpu
from jax.sharding import PartitionSpec as P

DEPTH = 8
XMAX = 64
LANES = 128
BLOCK_COLS = 512
CHUNK_ROWS = 32
GATHER_COLS = 1024
COST_SCALE = 1000
LOOKAHEAD = 2


def with_halo(cells, sides, width):
    for axis, dim in sides:
        count = lax.axis_size(axis)
        ends = count - 1
        head = lax.slice_in_dim(cells, 0, width, axis=dim)
        tail = lax.slice_in_dim(cells, cells.shape[dim] - width, cells.shape[dim], axis=dim)
        cells = jnp.concatenate(
            [
                lax.ppermute(tail, axis, [(i, (i + 1) % count) for i in range(ends)]),
                cells,
                lax.ppermute(head, axis, [((i + 1) % count, i) for i in range(ends)]),
            ],
            axis=dim,
        )
    return cells


def chunk_kernel(rs_ref, cs_ref, mid_ref, left_ref, psi_in, phi_in, psi_hbm, phi_hbm, slab_ref, out_vmem, sems,
                 *, first, last, epochs, hyps, rows_in, rows_out, chunk, out_lo, out_hi, col_base):
    del psi_in, phi_in
    side = left_ref.shape[-1]
    slab_rows = slab_ref.shape[1]
    slab_cols = slab_ref.shape[2]
    row_vregs = CHUNK_ROWS // 8
    width = out_hi - out_lo
    subs = []
    at = out_lo
    while at < out_hi:
        pieces = min(BLOCK_COLS // LANES, (out_hi - at) // LANES)
        subs.append((at, pieces))
        at += pieces * LANES
    copies = []
    for img, out_hbm in ((0, psi_hbm), (1, phi_hbm)):
        def convert(e, carry):
            if first:
                slab_ref[e, 0:rows_in, 0:side] = jnp.zeros((rows_in, side), jnp.float32)
            else:
                slab_ref[e, 0:rows_in, 0:side] = left_ref[e, img].astype(jnp.float32)
            slab_ref[e, 0:rows_in, side:side + chunk] = mid_ref[e, img].astype(jnp.float32)
            slab_ref[e, 0:rows_in, side + chunk:slab_cols] = jnp.zeros((rows_in, slab_cols - side - chunk), jnp.float32)
            slab_ref[e, rows_in:slab_rows, :] = jnp.zeros((slab_rows - rows_in, slab_cols), jnp.float32)
            return carry

        lax.fori_loop(0, epochs, convert, 0)

        for h in range(hyps):
            for rchunk in range(rows_out // CHUNK_ROWS):
                y0 = rchunk * CHUNK_ROWS
                for base_o, pieces in subs:
                    def add_epoch(e, acc, base_o=base_o, pieces=pieces):
                        start = DEPTH + rs_ref[e * hyps + h]
                        col = cs_ref[e * hyps + h]
                        a8 = start // 8
                        b8 = start - a8 * 8
                        q = (col + LANES) // LANES - 1
                        rem = col - q * LANES
                        row0 = pl.multiple_of(y0 + a8 * 8, 8)
                        lane0 = pl.multiple_of(base_o + q * LANES, LANES)
                        sub_mask = lax.broadcasted_iota(jnp.int32, (8, LANES), 0) >= b8
                        lane_mask = lax.broadcasted_iota(jnp.int32, (8, LANES), 1) >= rem
                        sub_shift = lax.rem(8 - b8, 8)
                        lane_shift = lax.rem(LANES - rem, LANES)
                        window = slab_ref.at[e, pl.ds(row0, CHUNK_ROWS + 8), pl.ds(lane0, (pieces + 1) * LANES)]
                        tiles = [
                            [window[8 * k:8 * k + 8, LANES * p:LANES * p + LANES] for p in range(pieces + 1)]
                            for k in range(row_vregs + 1)
                        ]
                        out = []
                        for k in range(row_vregs):
                            shifted = [
                                pltpu.roll(jnp.where(sub_mask, tiles[k][p], tiles[k + 1][p]), sub_shift, 0)
                                for p in range(pieces + 1)
                            ]
                            out.append([
                                acc[k][p]
                                + pltpu.roll(jnp.where(lane_mask, shifted[p], shifted[p + 1]), lane_shift, 1)
                                for p in range(pieces)
                            ])
                        return out

                    zero = [[jnp.zeros((8, LANES), jnp.float32) for _ in range(pieces)] for _ in range(row_vregs)]
                    acc = lax.fori_loop(0, epochs, add_epoch, zero, unroll=4)
                    for k in range(row_vregs):
                        for p in range(pieces):
                            lo = base_o - out_lo + LANES * p
                            out_vmem[img, h, pl.ds(y0 + 8 * k, 8), pl.ds(lo, LANES)] = acc[k][p]
        copy = pltpu.make_async_copy(
            out_vmem.at[img, :, :, pl.ds(0, width)],
            out_hbm.at[:, :, pl.ds(col_base + out_lo, width)],
            sems.at[img],
        )
        copy.start()
        copies.append(copy)
    for copy in copies:
        copy.wait()


def chunk_call(mid, left, rs, cs, psi_acc, phi_acc, *, index, count, rows_out):
    epochs, images, rows_in, chunk = mid.shape
    hyps = psi_acc.shape[0]
    cols = psi_acc.shape[2]
    side = 2 * LANES
    first = index == 0
    last = index == count - 1
    out_lo = side if first else side - LANES
    out_hi = side + chunk if last else side + chunk - LANES
    col_base = index * chunk - side
    kernel = functools.partial(
        chunk_kernel, first=first, last=last, epochs=epochs, hyps=hyps, rows_in=rows_in, rows_out=rows_out,
        chunk=chunk, out_lo=out_lo, out_hi=out_hi, col_base=col_base,
    )
    width = out_hi - out_lo
    vmem = pltpu.MemorySpace.VMEM
    smem = pltpu.MemorySpace.SMEM
    flops = 2 * epochs * hyps * images * rows_out * width * COST_SCALE
    return pl.pallas_call(
        kernel,
        out_shape=[jax.ShapeDtypeStruct((hyps, rows_out, cols), jnp.float32)] * 2,
        in_specs=[
            pl.BlockSpec(memory_space=smem),
            pl.BlockSpec(memory_space=smem),
            pl.BlockSpec(memory_space=vmem),
            pl.BlockSpec(memory_space=vmem),
            pl.BlockSpec(memory_space=pl.ANY),
            pl.BlockSpec(memory_space=pl.ANY),
        ],
        out_specs=[pl.BlockSpec(memory_space=pl.ANY), pl.BlockSpec(memory_space=pl.ANY)],
        scratch_shapes=[
            pltpu.VMEM((epochs, rows_in + 8, side + chunk + LANES), jnp.float32),
            pltpu.VMEM((images, hyps, rows_out, chunk + LANES), jnp.float32),
            pltpu.SemaphoreType.DMA((2,)),
        ],
        input_output_aliases={4: 0, 5: 1},
        compiler_params=pltpu.CompilerParams(vmem_limit_bytes=60 * 1024 * 1024),
        cost_estimate=pl.CostEstimate(
            flops=flops, transcendentals=0,
            bytes_accessed=(mid.size + left.size) * 2 + 2 * hyps * rows_out * width * 4,
        ),
        name=f"shift_stack_{index}",
    )(rs, cs, mid, left, psi_acc, phi_acc)


def body(psi, phi, row_shift, col_shift):
    row_count = psi.shape[1]
    col_count = psi.shape[2]
    hyp_count = row_shift.shape[1]
    images = jnp.stack([psi, phi], 1)
    extended = with_halo(images, (("sky", 2),), DEPTH)
    count = col_count // GATHER_COLS
    pieces = [extended[..., GATHER_COLS * i:GATHER_COLS * (i + 1)] for i in range(count)]
    rs = row_shift.reshape(-1)
    cs = col_shift.reshape(-1)
    psi_acc = jnp.zeros((hyp_count, row_count, col_count), jnp.float32)
    phi_acc = jnp.zeros((hyp_count, row_count, col_count), jnp.float32)
    gathered = [lax.all_gather(pieces[i], "epoch", axis=0, tiled=True) for i in range(min(LOOKAHEAD, count))]
    for i in range(count):
        mid = gathered[i]
        left = gathered[i - 1][..., GATHER_COLS - 2 * LANES:] if i > 0 else mid[..., :2 * LANES]
        psi_acc, phi_acc = chunk_call(mid, left, rs, cs, psi_acc, phi_acc, index=i, count=count, rows_out=row_count)
        ahead = i + LOOKAHEAD
        if ahead < count:
            piece, psi_acc, phi_acc = lax.optimization_barrier((pieces[ahead], psi_acc, phi_acc))
            gathered.append(lax.all_gather(piece, "epoch", axis=0, tiled=True))
    return psi_acc, phi_acc


def solution(mesh):
    return jax.shard_map(
        body,
        mesh=mesh,
        in_specs=(
            P("epoch", "sky", None),
            P("epoch", "sky", None),
            P(None, "epoch"),
            P(None, "epoch"),
        ),
        out_specs=(P("epoch", "sky", None), P("epoch", "sky", None)),
        check_vma=False,
    )
```

```python
import functools

import jax
import jax.numpy as jnp
from jax import lax
from jax.experimental import pallas as pl
from jax.experimental.pallas import tpu as pltpu
from jax.sharding import PartitionSpec as P

DEPTH = 8
XMAX = 64
LANES = 128
BLOCK_COLS = 512
CHUNK_ROWS = 32
SPLIT_BASE = 16
SPLIT = (10,)
COST_SCALE = 1000
LOOKAHEAD = 2


def with_halo(cells, sides, width):
    for axis, dim in sides:
        count = lax.axis_size(axis)
        ends = count - 1
        head = lax.slice_in_dim(cells, 0, width, axis=dim)
        tail = lax.slice_in_dim(cells, cells.shape[dim] - width, cells.shape[dim], axis=dim)
        cells = jnp.concatenate(
            [
                lax.ppermute(tail, axis, [(i, (i + 1) % count) for i in range(ends)]),
                cells,
                lax.ppermute(head, axis, [((i + 1) % count, i) for i in range(ends)]),
            ],
            axis=dim,
        )
    return cells


def chunk_kernel(rs_ref, cs_ref, mid_ref, left_ref, psi_in, phi_in, psi_hbm, phi_hbm, slab_ref, out_vmem, sems,
                 *, first, last, epochs, hyps, rows_in, rows_out, chunk, out_lo, out_hi, col_base):
    del psi_in, phi_in
    side = left_ref.shape[-1]
    slab_rows = slab_ref.shape[1]
    slab_cols = slab_ref.shape[2]
    row_vregs = CHUNK_ROWS // 8
    width = out_hi - out_lo
    subs = []
    at = out_lo
    while at < out_hi:
        pieces = min(BLOCK_COLS // LANES, (out_hi - at) // LANES)
        subs.append((at, pieces))
        at += pieces * LANES
    copies = []
    for img, out_hbm in ((0, psi_hbm), (1, phi_hbm)):
        def convert(e, carry):
            if first:
                slab_ref[e, 0:rows_in, 0:side] = jnp.zeros((rows_in, side), jnp.float32)
            else:
                slab_ref[e, 0:rows_in, 0:side] = left_ref[e, img].astype(jnp.float32)
            slab_ref[e, 0:rows_in, side:side + chunk] = mid_ref[e, img].astype(jnp.float32)
            slab_ref[e, 0:rows_in, side + chunk:slab_cols] = jnp.zeros((rows_in, slab_cols - side - chunk), jnp.float32)
            slab_ref[e, rows_in:slab_rows, :] = jnp.zeros((slab_rows - rows_in, slab_cols), jnp.float32)
            return carry

        lax.fori_loop(0, epochs, convert, 0)

        for h in range(hyps):
            for rchunk in range(rows_out // CHUNK_ROWS):
                y0 = rchunk * CHUNK_ROWS
                for base_o, pieces in subs:
                    def add_epoch(e, acc, base_o=base_o, pieces=pieces):
                        start = DEPTH + rs_ref[e * hyps + h]
                        col = cs_ref[e * hyps + h]
                        a8 = start // 8
                        b8 = start - a8 * 8
                        q = (col + LANES) // LANES - 1
                        rem = col - q * LANES
                        row0 = pl.multiple_of(y0 + a8 * 8, 8)
                        lane0 = pl.multiple_of(base_o + q * LANES, LANES)
                        sub_mask = lax.broadcasted_iota(jnp.int32, (8, LANES), 0) >= b8
                        lane_mask = lax.broadcasted_iota(jnp.int32, (8, LANES), 1) >= rem
                        sub_shift = lax.rem(8 - b8, 8)
                        lane_shift = lax.rem(LANES - rem, LANES)
                        window = slab_ref.at[e, pl.ds(row0, CHUNK_ROWS + 8), pl.ds(lane0, (pieces + 1) * LANES)]
                        tiles = [
                            [window[8 * k:8 * k + 8, LANES * p:LANES * p + LANES] for p in range(pieces + 1)]
                            for k in range(row_vregs + 1)
                        ]
                        out = []
                        for k in range(row_vregs):
                            shifted = [
                                pltpu.roll(jnp.where(sub_mask, tiles[k][p], tiles[k + 1][p]), sub_shift, 0)
                                for p in range(pieces + 1)
                            ]
                            out.append([
                                acc[k][p]
                                + pltpu.roll(jnp.where(lane_mask, shifted[p], shifted[p + 1]), lane_shift, 1)
                                for p in range(pieces)
                            ])
                        return out

                    zero = [[jnp.zeros((8, LANES), jnp.float32) for _ in range(pieces)] for _ in range(row_vregs)]
                    acc = lax.fori_loop(0, epochs, add_epoch, zero, unroll=4)
                    for k in range(row_vregs):
                        for p in range(pieces):
                            lo = base_o - out_lo + LANES * p
                            out_vmem[img, h, pl.ds(y0 + 8 * k, 8), pl.ds(lo, LANES)] = acc[k][p]
        copy = pltpu.make_async_copy(
            out_vmem.at[img, :, :, pl.ds(0, width)],
            out_hbm.at[:, :, pl.ds(col_base + out_lo, width)],
            sems.at[img],
        )
        copy.start()
        copies.append(copy)
    for copy in copies:
        copy.wait()


def chunk_call(mid, prev, rs, cs, psi_acc, phi_acc, *, index, count, start, rows_out):
    epochs, images, rows_in, chunk = mid.shape
    hyps = psi_acc.shape[0]
    cols = psi_acc.shape[2]
    side = 2 * LANES
    first = index == 0
    last = index == count - 1
    out_lo = side if first else side - LANES
    out_hi = side + chunk if last else side + chunk - LANES
    col_base = start - side
    kernel = functools.partial(
        chunk_kernel, first=first, last=last, epochs=epochs, hyps=hyps, rows_in=rows_in, rows_out=rows_out,
        chunk=chunk, out_lo=out_lo, out_hi=out_hi, col_base=col_base,
    )
    width = out_hi - out_lo
    prev_block = prev.shape[-1] // side - 1
    smem = pltpu.MemorySpace.SMEM
    flops = 2 * epochs * hyps * images * rows_out * width * COST_SCALE
    return pl.pallas_call(
        kernel,
        grid=(1,),
        out_shape=[jax.ShapeDtypeStruct((hyps, rows_out, cols), jnp.float32)] * 2,
        in_specs=[
            pl.BlockSpec(memory_space=smem),
            pl.BlockSpec(memory_space=smem),
            pl.BlockSpec((epochs, images, rows_in, chunk), lambda i: (0, 0, 0, 0)),
            pl.BlockSpec((epochs, images, rows_in, side), lambda i: (0, 0, 0, prev_block)),
            pl.BlockSpec(memory_space=pl.ANY),
            pl.BlockSpec(memory_space=pl.ANY),
        ],
        out_specs=[pl.BlockSpec(memory_space=pl.ANY), pl.BlockSpec(memory_space=pl.ANY)],
        scratch_shapes=[
            pltpu.VMEM((epochs, rows_in + 8, side + chunk + LANES), jnp.float32),
            pltpu.VMEM((images, hyps, rows_out, chunk + LANES), jnp.float32),
            pltpu.SemaphoreType.DMA((2,)),
        ],
        input_output_aliases={4: 0, 5: 1},
        compiler_params=pltpu.CompilerParams(vmem_limit_bytes=63 * 1024 * 1024),
        cost_estimate=pl.CostEstimate(
            flops=flops, transcendentals=0,
            bytes_accessed=mid.size * 2 + epochs * images * rows_in * side * 2 + 2 * hyps * rows_out * width * 4,
        ),
        name=f"shift_stack_{index}",
    )(rs, cs, mid, prev, psi_acc, phi_acc)


def body(psi, phi, row_shift, col_shift):
    row_count = psi.shape[1]
    col_count = psi.shape[2]
    hyp_count = row_shift.shape[1]
    images = jnp.stack([psi, phi], 1)
    extended = with_halo(images, (("sky", 2),), DEPTH)
    bounds = [0] + [b * col_count // SPLIT_BASE for b in SPLIT] + [col_count]
    count = len(bounds) - 1
    pieces = [extended[..., bounds[i]:bounds[i + 1]] for i in range(count)]
    rs = row_shift.reshape(-1)
    cs = col_shift.reshape(-1)
    psi_acc = jnp.zeros((hyp_count, row_count, col_count), jnp.float32)
    phi_acc = jnp.zeros((hyp_count, row_count, col_count), jnp.float32)
    gathered = [lax.all_gather(pieces[i], "epoch", axis=0, tiled=True) for i in range(min(LOOKAHEAD, count))]
    for i in range(count):
        mid = gathered[i]
        prev = gathered[i - 1] if i > 0 else mid
        psi_acc, phi_acc = chunk_call(
            mid, prev, rs, cs, psi_acc, phi_acc, index=i, count=count, start=bounds[i], rows_out=row_count
        )
        ahead = i + LOOKAHEAD
        if ahead < count:
            piece, psi_acc, phi_acc = lax.optimization_barrier((pieces[ahead], psi_acc, phi_acc))
            gathered.append(lax.all_gather(piece, "epoch", axis=0, tiled=True))
    return psi_acc, phi_acc


def solution(mesh):
    return jax.shard_map(
        body,
        mesh=mesh,
        in_specs=(
            P("epoch", "sky", None),
            P("epoch", "sky", None),
            P(None, "epoch"),
            P(None, "epoch"),
        ),
        out_specs=(P("epoch", "sky", None), P("epoch", "sky", None)),
        check_vma=False,
    )
```

```python
import functools

import jax
import jax.numpy as jnp
from jax import lax
from jax.experimental import pallas as pl
from jax.experimental.pallas import tpu as pltpu
from jax.sharding import PartitionSpec as P

DEPTH = 8
XMAX = 64
LANES = 128
BLOCK_COLS = 512
CHUNK_ROWS = 32
SPLIT_BASE = 16
SPLIT = (6, 12)
COST_SCALE = 1000
LOOKAHEAD = 2


def with_halo(cells, sides, width):
    for axis, dim in sides:
        count = lax.axis_size(axis)
        ends = count - 1
        head = lax.slice_in_dim(cells, 0, width, axis=dim)
        tail = lax.slice_in_dim(cells, cells.shape[dim] - width, cells.shape[dim], axis=dim)
        cells = jnp.concatenate(
            [
                lax.ppermute(tail, axis, [(i, (i + 1) % count) for i in range(ends)]),
                cells,
                lax.ppermute(head, axis, [((i + 1) % count, i) for i in range(ends)]),
            ],
            axis=dim,
        )
    return cells


def chunk_kernel(rs_ref, cs_ref, mid_ref, left_ref, psi_in, phi_in, psi_hbm, phi_hbm, slab_ref, out_vmem, sems,
                 *, first, last, epochs, hyps, rows_in, rows_out, chunk, out_lo, out_hi, col_base):
    side = left_ref.shape[-1]
    slab_rows = slab_ref.shape[1]
    slab_cols = slab_ref.shape[2]
    row_vregs = CHUNK_ROWS // 8
    width = out_hi - out_lo
    subs = []
    at = out_lo
    while at < out_hi:
        pieces = min(BLOCK_COLS // LANES, (out_hi - at) // LANES)
        subs.append((at, pieces))
        at += pieces * LANES
    copies = []
    for img, out_hbm in ((0, psi_hbm), (1, phi_hbm)):
        def convert(e, carry):
            if first:
                slab_ref[e, 0:rows_in, 0:side] = jnp.zeros((rows_in, side), jnp.float32)
            else:
                slab_ref[e, 0:rows_in, 0:side] = left_ref[e, img].astype(jnp.float32)
            slab_ref[e, 0:rows_in, side:side + chunk] = mid_ref[e, img].astype(jnp.float32)
            slab_ref[e, 0:rows_in, side + chunk:slab_cols] = jnp.zeros((rows_in, slab_cols - side - chunk), jnp.float32)
            slab_ref[e, rows_in:slab_rows, :] = jnp.zeros((slab_rows - rows_in, slab_cols), jnp.float32)
            return carry

        lax.fori_loop(0, epochs, convert, 0)

        for h in range(hyps):
            for rchunk in range(rows_out // CHUNK_ROWS):
                y0 = rchunk * CHUNK_ROWS
                for base_o, pieces in subs:
                    def add_epoch(e, acc, base_o=base_o, pieces=pieces):
                        start = DEPTH + rs_ref[e * hyps + h]
                        col = cs_ref[e * hyps + h]
                        a8 = start // 8
                        b8 = start - a8 * 8
                        q = (col + LANES) // LANES - 1
                        rem = col - q * LANES
                        row0 = pl.multiple_of(y0 + a8 * 8, 8)
                        lane0 = pl.multiple_of(base_o + q * LANES, LANES)
                        sub_mask = lax.broadcasted_iota(jnp.int32, (8, LANES), 0) >= b8
                        lane_mask = lax.broadcasted_iota(jnp.int32, (8, LANES), 1) >= rem
                        sub_shift = lax.rem(8 - b8, 8)
                        lane_shift = lax.rem(LANES - rem, LANES)
                        window = slab_ref.at[e, pl.ds(row0, CHUNK_ROWS + 8), pl.ds(lane0, (pieces + 1) * LANES)]
                        tiles = [
                            [window[8 * k:8 * k + 8, LANES * p:LANES * p + LANES] for p in range(pieces + 1)]
                            for k in range(row_vregs + 1)
                        ]
                        out = []
                        for k in range(row_vregs):
                            shifted = [
                                pltpu.roll(jnp.where(sub_mask, tiles[k][p], tiles[k + 1][p]), sub_shift, 0)
                                for p in range(pieces + 1)
                            ]
                            out.append([
                                acc[k][p]
                                + pltpu.roll(jnp.where(lane_mask, shifted[p], shifted[p + 1]), lane_shift, 1)
                                for p in range(pieces)
                            ])
                        return out

                    zero = [[jnp.zeros((8, LANES), jnp.float32) for _ in range(pieces)] for _ in range(row_vregs)]
                    acc = lax.fori_loop(0, epochs, add_epoch, zero, unroll=4)
                    for k in range(row_vregs):
                        for p in range(pieces):
                            lo = base_o - out_lo + LANES * p
                            out_vmem[img, h, pl.ds(y0 + 8 * k, 8), pl.ds(lo, LANES)] = acc[k][p]
        copy = pltpu.make_async_copy(
            out_vmem.at[img, :, :, pl.ds(0, width)],
            out_hbm.at[:, :, pl.ds(col_base + out_lo, width)],
            sems.at[img],
        )
        copy.start()
        copies.append(copy)
    for copy in copies:
        copy.wait()


def chunk_call(mid, prev, rs, cs, psi_acc, phi_acc, *, index, count, start, rows_out, hyps, cols):
    epochs, images, rows_in, chunk = mid.shape
    side = 2 * LANES
    first = index == 0
    last = index == count - 1
    out_lo = side if first else side - LANES
    out_hi = side + chunk if last else side + chunk - LANES
    col_base = start - side
    kernel = functools.partial(
        chunk_kernel, first=first, last=last, epochs=epochs, hyps=hyps, rows_in=rows_in, rows_out=rows_out,
        chunk=chunk, out_lo=out_lo, out_hi=out_hi, col_base=col_base,
    )
    if psi_acc is None:
        body_kernel = kernel

        def kernel(rs_ref, cs_ref, mid_ref, left_ref, psi_hbm, phi_hbm, *scratch):
            body_kernel(rs_ref, cs_ref, mid_ref, left_ref, None, None, psi_hbm, phi_hbm, *scratch)

    width = out_hi - out_lo
    prev_block = prev.shape[-1] // side - 1
    smem = pltpu.MemorySpace.SMEM
    flops = 2 * epochs * hyps * images * rows_out * width * COST_SCALE
    return pl.pallas_call(
        kernel,
        grid=(1,),
        out_shape=[jax.ShapeDtypeStruct((hyps, rows_out, cols), jnp.float32)] * 2,
        in_specs=[
            pl.BlockSpec(memory_space=smem),
            pl.BlockSpec(memory_space=smem),
            pl.BlockSpec((epochs, images, rows_in, chunk), lambda i: (0, 0, 0, 0)),
            pl.BlockSpec((epochs, images, rows_in, side), lambda i: (0, 0, 0, prev_block)),
        ] + ([] if psi_acc is None else [pl.BlockSpec(memory_space=pl.ANY)] * 2),
        out_specs=[pl.BlockSpec(memory_space=pl.ANY), pl.BlockSpec(memory_space=pl.ANY)],
        scratch_shapes=[
            pltpu.VMEM((epochs, rows_in + 8, side + chunk + LANES), jnp.float32),
            pltpu.VMEM((images, hyps, rows_out, chunk + LANES), jnp.float32),
            pltpu.SemaphoreType.DMA((2,)),
        ],
        input_output_aliases={} if psi_acc is None else {4: 0, 5: 1},
        compiler_params=pltpu.CompilerParams(vmem_limit_bytes=63 * 1024 * 1024),
        cost_estimate=pl.CostEstimate(
            flops=flops, transcendentals=0,
            bytes_accessed=mid.size * 2 + epochs * images * rows_in * side * 2 + 2 * hyps * rows_out * width * 4,
        ),
        name=f"shift_stack_{index}",
    )(rs, cs, mid, prev, *([] if psi_acc is None else [psi_acc, phi_acc]))


def body(psi, phi, row_shift, col_shift):
    row_count = psi.shape[1]
    col_count = psi.shape[2]
    hyp_count = row_shift.shape[1]
    images = jnp.stack([psi, phi], 1)
    extended = with_halo(images, (("sky", 2),), DEPTH)
    bounds = [0] + [b * col_count // SPLIT_BASE for b in SPLIT] + [col_count]
    count = len(bounds) - 1
    pieces = [extended[..., bounds[i]:bounds[i + 1]] for i in range(count)]
    rs = row_shift.reshape(-1)
    cs = col_shift.reshape(-1)
    psi_acc = phi_acc = None
    gathered = [lax.all_gather(pieces[i], "epoch", axis=0, tiled=True) for i in range(min(LOOKAHEAD, count))]
    for i in range(count):
        mid = gathered[i]
        prev = gathered[i - 1] if i > 0 else mid
        psi_acc, phi_acc = chunk_call(
            mid, prev, rs, cs, psi_acc, phi_acc, index=i, count=count, start=bounds[i], rows_out=row_count,
            hyps=hyp_count, cols=col_count,
        )
        ahead = i + LOOKAHEAD
        if ahead < count:
            piece, psi_acc, phi_acc = lax.optimization_barrier((pieces[ahead], psi_acc, phi_acc))
            gathered.append(lax.all_gather(piece, "epoch", axis=0, tiled=True))
    return psi_acc, phi_acc


def solution(mesh):
    return jax.shard_map(
        body,
        mesh=mesh,
        in_specs=(
            P("epoch", "sky", None),
            P("epoch", "sky", None),
            P(None, "epoch"),
            P(None, "epoch"),
        ),
        out_specs=(P("epoch", "sky", None), P("epoch", "sky", None)),
        check_vma=False,
    )
```

```python
import functools

import jax
import jax.numpy as jnp
from jax import lax
from jax.experimental import pallas as pl
from jax.experimental.pallas import tpu as pltpu
from jax.sharding import PartitionSpec as P

DEPTH = 8
XMAX = 64
LANES = 128
BLOCK_COLS = 512
CHUNK_ROWS = 32
SPLIT_BASE = 16
SPLIT = (8, 13)
COST_SCALE = 1000
LOOKAHEAD = 2


def with_halo(cells, sides, width):
    for axis, dim in sides:
        count = lax.axis_size(axis)
        ends = count - 1
        head = lax.slice_in_dim(cells, 0, width, axis=dim)
        tail = lax.slice_in_dim(cells, cells.shape[dim] - width, cells.shape[dim], axis=dim)
        cells = jnp.concatenate(
            [
                lax.ppermute(tail, axis, [(i, (i + 1) % count) for i in range(ends)]),
                cells,
                lax.ppermute(head, axis, [((i + 1) % count, i) for i in range(ends)]),
            ],
            axis=dim,
        )
    return cells


def chunk_kernel(rs_ref, cs_ref, mid_ref, left_ref, psi_in, phi_in, psi_hbm, phi_hbm, slab_ref, out_vmem, sems,
                 *, first, last, epochs, hyps, rows_in, rows_out, chunk, out_lo, out_hi, col_base):
    side = left_ref.shape[-1]
    slab_rows = slab_ref.shape[1]
    slab_cols = slab_ref.shape[2]
    row_vregs = CHUNK_ROWS // 8
    width = out_hi - out_lo
    subs = []
    at = out_lo
    while at < out_hi:
        pieces = min(BLOCK_COLS // LANES, (out_hi - at) // LANES)
        subs.append((at, pieces))
        at += pieces * LANES
    copies = []
    for img, out_hbm in ((0, psi_hbm), (1, phi_hbm)):
        def convert(e, carry):
            if first:
                slab_ref[e, 0:rows_in, 0:side] = jnp.zeros((rows_in, side), jnp.float32)
            else:
                slab_ref[e, 0:rows_in, 0:side] = left_ref[e, img].astype(jnp.float32)
            slab_ref[e, 0:rows_in, side:side + chunk] = mid_ref[e, img].astype(jnp.float32)
            slab_ref[e, 0:rows_in, side + chunk:slab_cols] = jnp.zeros((rows_in, slab_cols - side - chunk), jnp.float32)
            slab_ref[e, rows_in:slab_rows, :] = jnp.zeros((slab_rows - rows_in, slab_cols), jnp.float32)
            return carry

        lax.fori_loop(0, epochs, convert, 0)

        for h in range(hyps):
            for rchunk in range(rows_out // CHUNK_ROWS):
                y0 = rchunk * CHUNK_ROWS
                for base_o, pieces in subs:
                    def add_epoch(e, acc, base_o=base_o, pieces=pieces):
                        start = DEPTH + rs_ref[e * hyps + h]
                        col = cs_ref[e * hyps + h]
                        a8 = start // 8
                        b8 = start - a8 * 8
                        q = (col + LANES) // LANES - 1
                        rem = col - q * LANES
                        row0 = pl.multiple_of(y0 + a8 * 8, 8)
                        lane0 = pl.multiple_of(base_o + q * LANES, LANES)
                        sub_mask = lax.broadcasted_iota(jnp.int32, (8, LANES), 0) >= b8
                        lane_mask = lax.broadcasted_iota(jnp.int32, (8, LANES), 1) >= rem
                        sub_shift = lax.rem(8 - b8, 8)
                        lane_shift = lax.rem(LANES - rem, LANES)
                        window = slab_ref.at[e, pl.ds(row0, CHUNK_ROWS + 8), pl.ds(lane0, (pieces + 1) * LANES)]
                        tiles = [
                            [window[8 * k:8 * k + 8, LANES * p:LANES * p + LANES] for p in range(pieces + 1)]
                            for k in range(row_vregs + 1)
                        ]
                        out = []
                        for k in range(row_vregs):
                            shifted = [
                                pltpu.roll(jnp.where(sub_mask, tiles[k][p], tiles[k + 1][p]), sub_shift, 0)
                                for p in range(pieces + 1)
                            ]
                            out.append([
                                acc[k][p]
                                + pltpu.roll(jnp.where(lane_mask, shifted[p], shifted[p + 1]), lane_shift, 1)
                                for p in range(pieces)
                            ])
                        return out

                    zero = [[jnp.zeros((8, LANES), jnp.float32) for _ in range(pieces)] for _ in range(row_vregs)]
                    acc = lax.fori_loop(0, epochs, add_epoch, zero, unroll=4)
                    for k in range(row_vregs):
                        for p in range(pieces):
                            lo = base_o - out_lo + LANES * p
                            out_vmem[img, h, pl.ds(y0 + 8 * k, 8), pl.ds(lo, LANES)] = acc[k][p]
        copy = pltpu.make_async_copy(
            out_vmem.at[img, :, :, pl.ds(0, width)],
            out_hbm.at[:, :, pl.ds(col_base + out_lo, width)],
            sems.at[img],
        )
        copy.start()
        copies.append(copy)
    for copy in copies:
        copy.wait()


def chunk_call(mid, prev, rs, cs, psi_acc, phi_acc, *, index, count, start, rows_out, hyps, cols):
    epochs, images, rows_in, chunk = mid.shape
    side = 2 * LANES
    first = index == 0
    last = index == count - 1
    out_lo = side if first else side - LANES
    out_hi = side + chunk if last else side + chunk - LANES
    col_base = start - side
    kernel = functools.partial(
        chunk_kernel, first=first, last=last, epochs=epochs, hyps=hyps, rows_in=rows_in, rows_out=rows_out,
        chunk=chunk, out_lo=out_lo, out_hi=out_hi, col_base=col_base,
    )
    if psi_acc is None:
        body_kernel = kernel

        def kernel(rs_ref, cs_ref, mid_ref, left_ref, psi_hbm, phi_hbm, *scratch):
            body_kernel(rs_ref, cs_ref, mid_ref, left_ref, None, None, psi_hbm, phi_hbm, *scratch)

    width = out_hi - out_lo
    prev_block = prev.shape[-1] // side - 1
    smem = pltpu.MemorySpace.SMEM
    flops = 2 * epochs * hyps * images * rows_out * width * COST_SCALE
    return pl.pallas_call(
        kernel,
        grid=(1,),
        out_shape=[jax.ShapeDtypeStruct((hyps, rows_out, cols), jnp.float32)] * 2,
        in_specs=[
            pl.BlockSpec(memory_space=smem),
            pl.BlockSpec(memory_space=smem),
            pl.BlockSpec((epochs, images, rows_in, chunk), lambda i: (0, 0, 0, 0)),
            pl.BlockSpec((epochs, images, rows_in, side), lambda i: (0, 0, 0, prev_block)),
        ] + ([] if psi_acc is None else [pl.BlockSpec(memory_space=pl.ANY)] * 2),
        out_specs=[pl.BlockSpec(memory_space=pl.ANY), pl.BlockSpec(memory_space=pl.ANY)],
        scratch_shapes=[
            pltpu.VMEM((epochs, rows_in + 8, side + chunk + LANES), jnp.float32),
            pltpu.VMEM((images, hyps, rows_out, chunk + LANES), jnp.float32),
            pltpu.SemaphoreType.DMA((2,)),
        ],
        input_output_aliases={} if psi_acc is None else {4: 0, 5: 1},
        compiler_params=pltpu.CompilerParams(vmem_limit_bytes=63 * 1024 * 1024),
        cost_estimate=pl.CostEstimate(
            flops=flops, transcendentals=0,
            bytes_accessed=mid.size * 2 + epochs * images * rows_in * side * 2 + 2 * hyps * rows_out * width * 4,
        ),
        name=f"shift_stack_{index}",
    )(rs, cs, mid, prev, *([] if psi_acc is None else [psi_acc, phi_acc]))


def body(psi, phi, row_shift, col_shift):
    row_count = psi.shape[1]
    col_count = psi.shape[2]
    hyp_count = row_shift.shape[1]
    images = jnp.stack([psi, phi], 1)
    extended = with_halo(images, (("sky", 2),), DEPTH)
    bounds = [0] + [b * col_count // SPLIT_BASE for b in SPLIT] + [col_count]
    count = len(bounds) - 1
    pieces = [extended[..., bounds[i]:bounds[i + 1]] for i in range(count)]
    rs = row_shift.reshape(-1)
    cs = col_shift.reshape(-1)
    psi_acc = phi_acc = None
    gathered = [lax.all_gather(pieces[i], "epoch", axis=0, tiled=True) for i in range(min(LOOKAHEAD, count))]
    for i in range(count):
        mid = gathered[i]
        prev = gathered[i - 1] if i > 0 else mid
        psi_acc, phi_acc = chunk_call(
            mid, prev, rs, cs, psi_acc, phi_acc, index=i, count=count, start=bounds[i], rows_out=row_count,
            hyps=hyp_count, cols=col_count,
        )
        ahead = i + LOOKAHEAD
        if ahead < count:
            piece, psi_acc, phi_acc = lax.optimization_barrier((pieces[ahead], psi_acc, phi_acc))
            gathered.append(lax.all_gather(piece, "epoch", axis=0, tiled=True))
    return psi_acc, phi_acc


def solution(mesh):
    return jax.shard_map(
        body,
        mesh=mesh,
        in_specs=(
            P("epoch", "sky", None),
            P("epoch", "sky", None),
            P(None, "epoch"),
            P(None, "epoch"),
        ),
        out_specs=(P("epoch", "sky", None), P("epoch", "sky", None)),
        check_vma=False,
    )
```

```python
import functools

import jax
import jax.numpy as jnp
from jax import lax
from jax.experimental import pallas as pl
from jax.experimental.pallas import tpu as pltpu
from jax.sharding import PartitionSpec as P

DEPTH = 8
XMAX = 64
LANES = 128
BLOCK_COLS = 512
CHUNK_ROWS = 32
SPLIT_BASE = 16
SPLIT = (8, 13)
COST_SCALE = 1000
LOOKAHEAD = 2
UNROLL = 8


def with_halo(cells, sides, width):
    for axis, dim in sides:
        count = lax.axis_size(axis)
        ends = count - 1
        head = lax.slice_in_dim(cells, 0, width, axis=dim)
        tail = lax.slice_in_dim(cells, cells.shape[dim] - width, cells.shape[dim], axis=dim)
        cells = jnp.concatenate(
            [
                lax.ppermute(tail, axis, [(i, (i + 1) % count) for i in range(ends)]),
                cells,
                lax.ppermute(head, axis, [((i + 1) % count, i) for i in range(ends)]),
            ],
            axis=dim,
        )
    return cells


def chunk_kernel(rs_ref, cs_ref, mid_ref, left_ref, psi_in, phi_in, psi_hbm, phi_hbm, slab_ref, out_vmem, sems,
                 *, first, last, epochs, hyps, rows_in, rows_out, chunk, out_lo, out_hi, col_base):
    side = left_ref.shape[-1]
    slab_rows = slab_ref.shape[1]
    slab_cols = slab_ref.shape[2]
    row_vregs = CHUNK_ROWS // 8
    width = out_hi - out_lo
    subs = []
    at = out_lo
    while at < out_hi:
        pieces = min(BLOCK_COLS // LANES, (out_hi - at) // LANES)
        subs.append((at, pieces))
        at += pieces * LANES
    copies = []
    for img, out_hbm in ((0, psi_hbm), (1, phi_hbm)):
        def convert(e, carry):
            if first:
                slab_ref[e, 0:rows_in, 0:side] = jnp.zeros((rows_in, side), jnp.float32)
            else:
                slab_ref[e, 0:rows_in, 0:side] = left_ref[e, img].astype(jnp.float32)
            slab_ref[e, 0:rows_in, side:side + chunk] = mid_ref[e, img].astype(jnp.float32)
            slab_ref[e, 0:rows_in, side + chunk:slab_cols] = jnp.zeros((rows_in, slab_cols - side - chunk), jnp.float32)
            slab_ref[e, rows_in:slab_rows, :] = jnp.zeros((slab_rows - rows_in, slab_cols), jnp.float32)
            return carry

        lax.fori_loop(0, epochs, convert, 0)

        def one_hyp(h, carry):
            for rchunk in range(rows_out // CHUNK_ROWS):
                y0 = rchunk * CHUNK_ROWS
                for base_o, pieces in subs:
                    def add_epoch(e, acc, base_o=base_o, pieces=pieces):
                        start = DEPTH + rs_ref[e * hyps + h]
                        col = cs_ref[e * hyps + h]
                        a8 = start // 8
                        b8 = start - a8 * 8
                        q = (col + LANES) // LANES - 1
                        rem = col - q * LANES
                        row0 = pl.multiple_of(y0 + a8 * 8, 8)
                        lane0 = pl.multiple_of(base_o + q * LANES, LANES)
                        sub_mask = lax.broadcasted_iota(jnp.int32, (8, LANES), 0) >= b8
                        lane_mask = lax.broadcasted_iota(jnp.int32, (8, LANES), 1) >= rem
                        sub_shift = lax.rem(8 - b8, 8)
                        lane_shift = lax.rem(LANES - rem, LANES)
                        window = slab_ref.at[e, pl.ds(row0, CHUNK_ROWS + 8), pl.ds(lane0, (pieces + 1) * LANES)]
                        tiles = [
                            [window[8 * k:8 * k + 8, LANES * p:LANES * p + LANES] for p in range(pieces + 1)]
                            for k in range(row_vregs + 1)
                        ]
                        out = []
                        for k in range(row_vregs):
                            shifted = [
                                pltpu.roll(jnp.where(sub_mask, tiles[k][p], tiles[k + 1][p]), sub_shift, 0)
                                for p in range(pieces + 1)
                            ]
                            out.append([
                                acc[k][p]
                                + pltpu.roll(jnp.where(lane_mask, shifted[p], shifted[p + 1]), lane_shift, 1)
                                for p in range(pieces)
                            ])
                        return out

                    zero = [[jnp.zeros((8, LANES), jnp.float32) for _ in range(pieces)] for _ in range(row_vregs)]
                    acc = lax.fori_loop(0, epochs, add_epoch, zero, unroll=UNROLL)
                    for k in range(row_vregs):
                        for p in range(pieces):
                            lo = base_o - out_lo + LANES * p
                            out_vmem[img, h, pl.ds(y0 + 8 * k, 8), pl.ds(lo, LANES)] = acc[k][p]
            return carry

        lax.fori_loop(0, hyps, one_hyp, 0)
        copy = pltpu.make_async_copy(
            out_vmem.at[img, :, :, pl.ds(0, width)],
            out_hbm.at[:, :, pl.ds(col_base + out_lo, width)],
            sems.at[img],
        )
        copy.start()
        copies.append(copy)
    for copy in copies:
        copy.wait()


def chunk_call(mid, prev, rs, cs, psi_acc, phi_acc, *, index, count, start, rows_out, hyps, cols):
    epochs, images, rows_in, chunk = mid.shape
    side = 2 * LANES
    first = index == 0
    last = index == count - 1
    out_lo = side if first else side - LANES
    out_hi = side + chunk if last else side + chunk - LANES
    col_base = start - side
    kernel = functools.partial(
        chunk_kernel, first=first, last=last, epochs=epochs, hyps=hyps, rows_in=rows_in, rows_out=rows_out,
        chunk=chunk, out_lo=out_lo, out_hi=out_hi, col_base=col_base,
    )
    if psi_acc is None:
        body_kernel = kernel

        def kernel(rs_ref, cs_ref, mid_ref, left_ref, psi_hbm, phi_hbm, *scratch):
            body_kernel(rs_ref, cs_ref, mid_ref, left_ref, None, None, psi_hbm, phi_hbm, *scratch)

    width = out_hi - out_lo
    prev_block = prev.shape[-1] // side - 1
    smem = pltpu.MemorySpace.SMEM
    flops = 2 * epochs * hyps * images * rows_out * width * COST_SCALE
    return pl.pallas_call(
        kernel,
        grid=(1,),
        out_shape=[jax.ShapeDtypeStruct((hyps, rows_out, cols), jnp.float32)] * 2,
        in_specs=[
            pl.BlockSpec(memory_space=smem),
            pl.BlockSpec(memory_space=smem),
            pl.BlockSpec((epochs, images, rows_in, chunk), lambda i: (0, 0, 0, 0)),
            pl.BlockSpec((epochs, images, rows_in, side), lambda i: (0, 0, 0, prev_block)),
        ] + ([] if psi_acc is None else [pl.BlockSpec(memory_space=pl.ANY)] * 2),
        out_specs=[pl.BlockSpec(memory_space=pl.ANY), pl.BlockSpec(memory_space=pl.ANY)],
        scratch_shapes=[
            pltpu.VMEM((epochs, rows_in + 8, side + chunk + LANES), jnp.float32),
            pltpu.VMEM((images, hyps, rows_out, chunk + LANES), jnp.float32),
            pltpu.SemaphoreType.DMA((2,)),
        ],
        input_output_aliases={} if psi_acc is None else {4: 0, 5: 1},
        compiler_params=pltpu.CompilerParams(vmem_limit_bytes=63 * 1024 * 1024),
        cost_estimate=pl.CostEstimate(
            flops=flops, transcendentals=0,
            bytes_accessed=mid.size * 2 + epochs * images * rows_in * side * 2 + 2 * hyps * rows_out * width * 4,
        ),
        name=f"shift_stack_{index}",
    )(rs, cs, mid, prev, *([] if psi_acc is None else [psi_acc, phi_acc]))


def body(psi, phi, row_shift, col_shift):
    row_count = psi.shape[1]
    col_count = psi.shape[2]
    hyp_count = row_shift.shape[1]
    images = jnp.stack([psi, phi], 1)
    extended = with_halo(images, (("sky", 2),), DEPTH)
    bounds = [0] + [b * col_count // SPLIT_BASE for b in SPLIT] + [col_count]
    count = len(bounds) - 1
    pieces = [extended[..., bounds[i]:bounds[i + 1]] for i in range(count)]
    rs = row_shift.reshape(-1)
    cs = col_shift.reshape(-1)
    psi_acc = phi_acc = None
    gathered = [lax.all_gather(pieces[i], "epoch", axis=0, tiled=True) for i in range(min(LOOKAHEAD, count))]
    for i in range(count):
        mid = gathered[i]
        prev = gathered[i - 1] if i > 0 else mid
        psi_acc, phi_acc = chunk_call(
            mid, prev, rs, cs, psi_acc, phi_acc, index=i, count=count, start=bounds[i], rows_out=row_count,
            hyps=hyp_count, cols=col_count,
        )
        ahead = i + LOOKAHEAD
        if ahead < count:
            piece, psi_acc, phi_acc = lax.optimization_barrier((pieces[ahead], psi_acc, phi_acc))
            gathered.append(lax.all_gather(piece, "epoch", axis=0, tiled=True))
    return psi_acc, phi_acc


def solution(mesh):
    return jax.shard_map(
        body,
        mesh=mesh,
        in_specs=(
            P("epoch", "sky", None),
            P("epoch", "sky", None),
            P(None, "epoch"),
            P(None, "epoch"),
        ),
        out_specs=(P("epoch", "sky", None), P("epoch", "sky", None)),
        check_vma=False,
    )
```

```python
import functools

import jax
import jax.numpy as jnp
from jax import lax
from jax.experimental import pallas as pl
from jax.experimental.pallas import tpu as pltpu
from jax.sharding import PartitionSpec as P

DEPTH = 8
XMAX = 64
LANES = 128
BLOCK_COLS = 512
CHUNK_ROWS = 32
SPLIT_BASE = 16
SPLIT = (10,)
COST_SCALE = 1000
LOOKAHEAD = 2
UNROLL = 8


def with_halo(cells, sides, width):
    for axis, dim in sides:
        count = lax.axis_size(axis)
        ends = count - 1
        head = lax.slice_in_dim(cells, 0, width, axis=dim)
        tail = lax.slice_in_dim(cells, cells.shape[dim] - width, cells.shape[dim], axis=dim)
        cells = jnp.concatenate(
            [
                lax.ppermute(tail, axis, [(i, (i + 1) % count) for i in range(ends)]),
                cells,
                lax.ppermute(head, axis, [((i + 1) % count, i) for i in range(ends)]),
            ],
            axis=dim,
        )
    return cells


def chunk_kernel(rs_ref, cs_ref, mid_ref, left_ref, psi_in, phi_in, psi_hbm, phi_hbm, slab_ref, out_vmem, sems,
                 *, first, last, epochs, hyps, rows_in, rows_out, chunk, out_lo, out_hi, col_base):
    side = left_ref.shape[-1]
    slab_rows = slab_ref.shape[1]
    slab_cols = slab_ref.shape[2]
    row_vregs = CHUNK_ROWS // 8
    width = out_hi - out_lo
    subs = []
    at = out_lo
    while at < out_hi:
        pieces = min(BLOCK_COLS // LANES, (out_hi - at) // LANES)
        subs.append((at, pieces))
        at += pieces * LANES
    copies = []
    for img, out_hbm in ((0, psi_hbm), (1, phi_hbm)):
        def convert(e, carry):
            if first:
                slab_ref[e, 0:rows_in, 0:side] = jnp.zeros((rows_in, side), jnp.float32)
            else:
                slab_ref[e, 0:rows_in, 0:side] = left_ref[e, img].astype(jnp.float32)
            slab_ref[e, 0:rows_in, side:side + chunk] = mid_ref[e, img].astype(jnp.float32)
            slab_ref[e, 0:rows_in, side + chunk:slab_cols] = jnp.zeros((rows_in, slab_cols - side - chunk), jnp.float32)
            slab_ref[e, rows_in:slab_rows, :] = jnp.zeros((slab_rows - rows_in, slab_cols), jnp.float32)
            return carry

        lax.fori_loop(0, epochs, convert, 0)

        def one_hyp(h, carry):
            for rchunk in range(rows_out // CHUNK_ROWS):
                y0 = rchunk * CHUNK_ROWS
                for base_o, pieces in subs:
                    def add_epoch(e, acc, base_o=base_o, pieces=pieces):
                        start = DEPTH + rs_ref[e * hyps + h]
                        col = cs_ref[e * hyps + h]
                        a8 = start // 8
                        b8 = start - a8 * 8
                        q = (col + LANES) // LANES - 1
                        rem = col - q * LANES
                        row0 = pl.multiple_of(y0 + a8 * 8, 8)
                        lane0 = pl.multiple_of(base_o + q * LANES, LANES)
                        sub_mask = lax.broadcasted_iota(jnp.int32, (8, LANES), 0) >= b8
                        lane_mask = lax.broadcasted_iota(jnp.int32, (8, LANES), 1) >= rem
                        sub_shift = lax.rem(8 - b8, 8)
                        lane_shift = lax.rem(LANES - rem, LANES)
                        window = slab_ref.at[e, pl.ds(row0, CHUNK_ROWS + 8), pl.ds(lane0, (pieces + 1) * LANES)]
                        tiles = [
                            [window[8 * k:8 * k + 8, LANES * p:LANES * p + LANES] for p in range(pieces + 1)]
                            for k in range(row_vregs + 1)
                        ]
                        out = []
                        for k in range(row_vregs):
                            shifted = [
                                pltpu.roll(jnp.where(sub_mask, tiles[k][p], tiles[k + 1][p]), sub_shift, 0)
                                for p in range(pieces + 1)
                            ]
                            out.append([
                                acc[k][p]
                                + pltpu.roll(jnp.where(lane_mask, shifted[p], shifted[p + 1]), lane_shift, 1)
                                for p in range(pieces)
                            ])
                        return out

                    zero = [[jnp.zeros((8, LANES), jnp.float32) for _ in range(pieces)] for _ in range(row_vregs)]
                    acc = lax.fori_loop(0, epochs, add_epoch, zero, unroll=UNROLL)
                    for k in range(row_vregs):
                        for p in range(pieces):
                            lo = base_o - out_lo + LANES * p
                            out_vmem[img, h, pl.ds(y0 + 8 * k, 8), pl.ds(lo, LANES)] = acc[k][p]
            return carry

        lax.fori_loop(0, hyps, one_hyp, 0)
        copy = pltpu.make_async_copy(
            out_vmem.at[img, :, :, pl.ds(0, width)],
            out_hbm.at[:, :, pl.ds(col_base + out_lo, width)],
            sems.at[img],
        )
        copy.start()
        copies.append(copy)
    for copy in copies:
        copy.wait()


def chunk_call(mid, prev, rs, cs, psi_acc, phi_acc, *, index, count, start, rows_out, hyps, cols):
    epochs, images, rows_in, chunk = mid.shape
    side = 2 * LANES
    first = index == 0
    last = index == count - 1
    out_lo = side if first else side - LANES
    out_hi = side + chunk if last else side + chunk - LANES
    col_base = start - side
    kernel = functools.partial(
        chunk_kernel, first=first, last=last, epochs=epochs, hyps=hyps, rows_in=rows_in, rows_out=rows_out,
        chunk=chunk, out_lo=out_lo, out_hi=out_hi, col_base=col_base,
    )
    if psi_acc is None:
        body_kernel = kernel

        def kernel(rs_ref, cs_ref, mid_ref, left_ref, psi_hbm, phi_hbm, *scratch):
            body_kernel(rs_ref, cs_ref, mid_ref, left_ref, None, None, psi_hbm, phi_hbm, *scratch)

    width = out_hi - out_lo
    prev_block = prev.shape[-1] // side - 1
    smem = pltpu.MemorySpace.SMEM
    flops = 2 * epochs * hyps * images * rows_out * width * COST_SCALE
    return pl.pallas_call(
        kernel,
        grid=(1,),
        out_shape=[jax.ShapeDtypeStruct((hyps, rows_out, cols), jnp.float32)] * 2,
        in_specs=[
            pl.BlockSpec(memory_space=smem),
            pl.BlockSpec(memory_space=smem),
            pl.BlockSpec((epochs, images, rows_in, chunk), lambda i: (0, 0, 0, 0)),
            pl.BlockSpec((epochs, images, rows_in, side), lambda i: (0, 0, 0, prev_block)),
        ] + ([] if psi_acc is None else [pl.BlockSpec(memory_space=pl.ANY)] * 2),
        out_specs=[pl.BlockSpec(memory_space=pl.ANY), pl.BlockSpec(memory_space=pl.ANY)],
        scratch_shapes=[
            pltpu.VMEM((epochs, rows_in + 8, side + chunk + LANES), jnp.float32),
            pltpu.VMEM((images, hyps, rows_out, chunk + LANES), jnp.float32),
            pltpu.SemaphoreType.DMA((2,)),
        ],
        input_output_aliases={} if psi_acc is None else {4: 0, 5: 1},
        compiler_params=pltpu.CompilerParams(vmem_limit_bytes=63 * 1024 * 1024),
        cost_estimate=pl.CostEstimate(
            flops=flops, transcendentals=0,
            bytes_accessed=mid.size * 2 + epochs * images * rows_in * side * 2 + 2 * hyps * rows_out * width * 4,
        ),
        name=f"shift_stack_{index}",
    )(rs, cs, mid, prev, *([] if psi_acc is None else [psi_acc, phi_acc]))


def body(psi, phi, row_shift, col_shift):
    row_count = psi.shape[1]
    col_count = psi.shape[2]
    hyp_count = row_shift.shape[1]
    images = jnp.stack([psi, phi], 1)
    extended = with_halo(images, (("sky", 2),), DEPTH)
    bounds = [0] + [b * col_count // SPLIT_BASE for b in SPLIT] + [col_count]
    count = len(bounds) - 1
    pieces = [extended[..., bounds[i]:bounds[i + 1]] for i in range(count)]
    rs = row_shift.reshape(-1)
    cs = col_shift.reshape(-1)
    psi_acc = phi_acc = None
    gathered = [lax.all_gather(pieces[i], "epoch", axis=0, tiled=True) for i in range(min(LOOKAHEAD, count))]
    for i in range(count):
        mid = gathered[i]
        prev = gathered[i - 1] if i > 0 else mid
        psi_acc, phi_acc = chunk_call(
            mid, prev, rs, cs, psi_acc, phi_acc, index=i, count=count, start=bounds[i], rows_out=row_count,
            hyps=hyp_count, cols=col_count,
        )
        ahead = i + LOOKAHEAD
        if ahead < count:
            piece, psi_acc, phi_acc = lax.optimization_barrier((pieces[ahead], psi_acc, phi_acc))
            gathered.append(lax.all_gather(piece, "epoch", axis=0, tiled=True))
    return psi_acc, phi_acc


def solution(mesh):
    return jax.shard_map(
        body,
        mesh=mesh,
        in_specs=(
            P("epoch", "sky", None),
            P("epoch", "sky", None),
            P(None, "epoch"),
            P(None, "epoch"),
        ),
        out_specs=(P("epoch", "sky", None), P("epoch", "sky", None)),
        check_vma=False,
    )
```

```python
import functools

import jax
import jax.numpy as jnp
from jax import lax
from jax.experimental import pallas as pl
from jax.experimental.pallas import tpu as pltpu
from jax.sharding import PartitionSpec as P

DEPTH = 8
XMAX = 64
LANES = 128
BLOCK_COLS = 512
CHUNK_ROWS = 32
SPLIT_BASE = 16
SPLIT = (10,)
COST_SCALE = 1000
LOOKAHEAD = 2
UNROLL = 8


def with_halo(cells, sides, width):
    for axis, dim in sides:
        count = lax.axis_size(axis)
        ends = count - 1
        head = lax.slice_in_dim(cells, 0, width, axis=dim)
        tail = lax.slice_in_dim(cells, cells.shape[dim] - width, cells.shape[dim], axis=dim)
        cells = jnp.concatenate(
            [
                lax.ppermute(tail, axis, [(i, (i + 1) % count) for i in range(ends)]),
                cells,
                lax.ppermute(head, axis, [((i + 1) % count, i) for i in range(ends)]),
            ],
            axis=dim,
        )
    return cells


def chunk_kernel(rs_ref, cs_ref, mid_ref, left_ref, psi_in, phi_in, psi_hbm, phi_hbm, slab_ref, out_vmem, sems,
                 *, first, last, epochs, hyps, rows_in, rows_out, chunk, out_lo, out_hi, col_base):
    side = left_ref.shape[-1]
    slab_rows = slab_ref.shape[1]
    slab_cols = slab_ref.shape[2]
    row_vregs = CHUNK_ROWS // 8
    width = out_hi - out_lo
    subs = []
    at = out_lo
    while at < out_hi:
        pieces = min(BLOCK_COLS // LANES, (out_hi - at) // LANES)
        subs.append((at, pieces))
        at += pieces * LANES
    img = pl.program_id(0)
    e_now = pl.program_id(1)
    if first:
        slab_ref[e_now, 0:rows_in, 0:side] = jnp.zeros((rows_in, side), jnp.float32)
    else:
        slab_ref[e_now, 0:rows_in, 0:side] = left_ref[0, 0].astype(jnp.float32)
    slab_ref[e_now, 0:rows_in, side:side + chunk] = mid_ref[0, 0].astype(jnp.float32)
    slab_ref[e_now, 0:rows_in, side + chunk:slab_cols] = jnp.zeros((rows_in, slab_cols - side - chunk), jnp.float32)
    slab_ref[e_now, rows_in:slab_rows, :] = jnp.zeros((slab_rows - rows_in, slab_cols), jnp.float32)

    @pl.when(e_now == epochs - 1)
    def _():
        def one_hyp(h, carry):
            for rchunk in range(rows_out // CHUNK_ROWS):
                y0 = rchunk * CHUNK_ROWS
                for base_o, pieces in subs:
                    def add_epoch(e, acc, base_o=base_o, pieces=pieces):
                        start = DEPTH + rs_ref[e * hyps + h]
                        col = cs_ref[e * hyps + h]
                        a8 = start // 8
                        b8 = start - a8 * 8
                        q = (col + LANES) // LANES - 1
                        rem = col - q * LANES
                        row0 = pl.multiple_of(y0 + a8 * 8, 8)
                        lane0 = pl.multiple_of(base_o + q * LANES, LANES)
                        sub_mask = lax.broadcasted_iota(jnp.int32, (8, LANES), 0) >= b8
                        lane_mask = lax.broadcasted_iota(jnp.int32, (8, LANES), 1) >= rem
                        sub_shift = lax.rem(8 - b8, 8)
                        lane_shift = lax.rem(LANES - rem, LANES)
                        window = slab_ref.at[e, pl.ds(row0, CHUNK_ROWS + 8), pl.ds(lane0, (pieces + 1) * LANES)]
                        tiles = [
                            [window[8 * k:8 * k + 8, LANES * p:LANES * p + LANES] for p in range(pieces + 1)]
                            for k in range(row_vregs + 1)
                        ]
                        out = []
                        for k in range(row_vregs):
                            shifted = [
                                pltpu.roll(jnp.where(sub_mask, tiles[k][p], tiles[k + 1][p]), sub_shift, 0)
                                for p in range(pieces + 1)
                            ]
                            out.append([
                                acc[k][p]
                                + pltpu.roll(jnp.where(lane_mask, shifted[p], shifted[p + 1]), lane_shift, 1)
                                for p in range(pieces)
                            ])
                        return out

                    zero = [[jnp.zeros((8, LANES), jnp.float32) for _ in range(pieces)] for _ in range(row_vregs)]
                    acc = lax.fori_loop(0, epochs, add_epoch, zero, unroll=UNROLL)
                    for k in range(row_vregs):
                        for p in range(pieces):
                            lo = base_o - out_lo + LANES * p
                            out_vmem[img, h, pl.ds(y0 + 8 * k, 8), pl.ds(lo, LANES)] = acc[k][p]
            return carry

        lax.fori_loop(0, hyps, one_hyp, 0)
        for index, out_hbm in enumerate((psi_hbm, phi_hbm)):
            @pl.when(img == index)
            def _():
                copy = pltpu.make_async_copy(
                    out_vmem.at[index, :, :, pl.ds(0, width)],
                    out_hbm.at[:, :, pl.ds(col_base + out_lo, width)],
                    sems.at[index],
                )
                copy.start()
                copy.wait()


def chunk_call(mid, prev, rs, cs, psi_acc, phi_acc, *, index, count, start, rows_out, hyps, cols):
    epochs, images, rows_in, chunk = mid.shape
    side = 2 * LANES
    first = index == 0
    last = index == count - 1
    out_lo = side if first else side - LANES
    out_hi = side + chunk if last else side + chunk - LANES
    col_base = start - side
    kernel = functools.partial(
        chunk_kernel, first=first, last=last, epochs=epochs, hyps=hyps, rows_in=rows_in, rows_out=rows_out,
        chunk=chunk, out_lo=out_lo, out_hi=out_hi, col_base=col_base,
    )
    if psi_acc is None:
        body_kernel = kernel

        def kernel(rs_ref, cs_ref, mid_ref, left_ref, psi_hbm, phi_hbm, *scratch):
            body_kernel(rs_ref, cs_ref, mid_ref, left_ref, None, None, psi_hbm, phi_hbm, *scratch)

    width = out_hi - out_lo
    prev_block = prev.shape[-1] // side - 1
    smem = pltpu.MemorySpace.SMEM
    flops = 2 * epochs * hyps * images * rows_out * width * COST_SCALE
    return pl.pallas_call(
        kernel,
        grid=(images, epochs),
        out_shape=[jax.ShapeDtypeStruct((hyps, rows_out, cols), jnp.float32)] * 2,
        in_specs=[
            pl.BlockSpec(memory_space=smem),
            pl.BlockSpec(memory_space=smem),
            pl.BlockSpec((1, 1, rows_in, chunk), lambda i, e: (e, i, 0, 0)),
            pl.BlockSpec((1, 1, rows_in, side), lambda i, e: (e, i, 0, prev_block)),
        ] + ([] if psi_acc is None else [pl.BlockSpec(memory_space=pl.ANY)] * 2),
        out_specs=[pl.BlockSpec(memory_space=pl.ANY), pl.BlockSpec(memory_space=pl.ANY)],
        scratch_shapes=[
            pltpu.VMEM((epochs, rows_in + 8, side + chunk + LANES), jnp.float32),
            pltpu.VMEM((images, hyps, rows_out, chunk + LANES), jnp.float32),
            pltpu.SemaphoreType.DMA((2,)),
        ],
        input_output_aliases={} if psi_acc is None else {4: 0, 5: 1},
        compiler_params=pltpu.CompilerParams(vmem_limit_bytes=63 * 1024 * 1024),
        cost_estimate=pl.CostEstimate(
            flops=flops, transcendentals=0,
            bytes_accessed=mid.size * 2 + epochs * images * rows_in * side * 2 + 2 * hyps * rows_out * width * 4,
        ),
        name=f"shift_stack_{index}",
    )(rs, cs, mid, prev, *([] if psi_acc is None else [psi_acc, phi_acc]))


def body(psi, phi, row_shift, col_shift):
    row_count = psi.shape[1]
    col_count = psi.shape[2]
    hyp_count = row_shift.shape[1]
    images = jnp.stack([psi, phi], 1)
    extended = with_halo(images, (("sky", 2),), DEPTH)
    bounds = [0] + [b * col_count // SPLIT_BASE for b in SPLIT] + [col_count]
    count = len(bounds) - 1
    pieces = [extended[..., bounds[i]:bounds[i + 1]] for i in range(count)]
    rs = row_shift.reshape(-1)
    cs = col_shift.reshape(-1)
    psi_acc = phi_acc = None
    gathered = [lax.all_gather(pieces[i], "epoch", axis=0, tiled=True) for i in range(min(LOOKAHEAD, count))]
    for i in range(count):
        mid = gathered[i]
        prev = gathered[i - 1] if i > 0 else mid
        psi_acc, phi_acc = chunk_call(
            mid, prev, rs, cs, psi_acc, phi_acc, index=i, count=count, start=bounds[i], rows_out=row_count,
            hyps=hyp_count, cols=col_count,
        )
        ahead = i + LOOKAHEAD
        if ahead < count:
            piece, psi_acc, phi_acc = lax.optimization_barrier((pieces[ahead], psi_acc, phi_acc))
            gathered.append(lax.all_gather(piece, "epoch", axis=0, tiled=True))
    return psi_acc, phi_acc


def solution(mesh):
    return jax.shard_map(
        body,
        mesh=mesh,
        in_specs=(
            P("epoch", "sky", None),
            P("epoch", "sky", None),
            P(None, "epoch"),
            P(None, "epoch"),
        ),
        out_specs=(P("epoch", "sky", None), P("epoch", "sky", None)),
        check_vma=False,
    )
```

```python
import functools

import jax
import jax.numpy as jnp
from jax import lax
from jax.experimental import pallas as pl
from jax.experimental.pallas import tpu as pltpu
from jax.sharding import PartitionSpec as P

DEPTH = 8
XMAX = 64
LANES = 128
BLOCK_COLS = 512
CHUNK_ROWS = 32
SPLIT_BASE = 16
SPLIT = (10,)
COST_SCALE = 1000
LOOKAHEAD = 2
UNROLL = 8


def with_halo(cells, sides, width):
    for axis, dim in sides:
        count = lax.axis_size(axis)
        ends = count - 1
        head = lax.slice_in_dim(cells, 0, width, axis=dim)
        tail = lax.slice_in_dim(cells, cells.shape[dim] - width, cells.shape[dim], axis=dim)
        cells = jnp.concatenate(
            [
                lax.ppermute(tail, axis, [(i, (i + 1) % count) for i in range(ends)]),
                cells,
                lax.ppermute(head, axis, [((i + 1) % count, i) for i in range(ends)]),
            ],
            axis=dim,
        )
    return cells


def chunk_kernel(rs_ref, cs_ref, mid_ref, left_ref, psi_in, phi_in, psi_hbm, phi_hbm, slab_ref, out_vmem, sems,
                 *, first, last, epochs, hyps, rows_in, rows_out, chunk, out_lo, out_hi, col_base):
    side = left_ref.shape[-1]
    slab_rows = slab_ref.shape[1]
    slab_cols = slab_ref.shape[2]
    row_vregs = CHUNK_ROWS // 8
    width = out_hi - out_lo
    subs = []
    at = out_lo
    while at < out_hi:
        pieces = min(BLOCK_COLS // LANES, (out_hi - at) // LANES)
        subs.append((at, pieces))
        at += pieces * LANES
    img = pl.program_id(0)
    if True:
        def convert(e, carry):
            if first:
                slab_ref[e, 0:rows_in, 0:side] = jnp.zeros((rows_in, side), jnp.float32)
            else:
                slab_ref[e, 0:rows_in, 0:side] = left_ref[e, 0].astype(jnp.float32)
            slab_ref[e, 0:rows_in, side:side + chunk] = mid_ref[e, 0].astype(jnp.float32)
            slab_ref[e, 0:rows_in, side + chunk:slab_cols] = jnp.zeros((rows_in, slab_cols - side - chunk), jnp.float32)
            slab_ref[e, rows_in:slab_rows, :] = jnp.zeros((slab_rows - rows_in, slab_cols), jnp.float32)
            return carry

        lax.fori_loop(0, epochs, convert, 0)

        def one_hyp(h, carry):
            for rchunk in range(rows_out // CHUNK_ROWS):
                y0 = rchunk * CHUNK_ROWS
                for base_o, pieces in subs:
                    def add_epoch(e, acc, base_o=base_o, pieces=pieces):
                        start = DEPTH + rs_ref[e * hyps + h]
                        col = cs_ref[e * hyps + h]
                        a8 = start // 8
                        b8 = start - a8 * 8
                        q = (col + LANES) // LANES - 1
                        rem = col - q * LANES
                        row0 = pl.multiple_of(y0 + a8 * 8, 8)
                        lane0 = pl.multiple_of(base_o + q * LANES, LANES)
                        sub_mask = lax.broadcasted_iota(jnp.int32, (8, LANES), 0) >= b8
                        lane_mask = lax.broadcasted_iota(jnp.int32, (8, LANES), 1) >= rem
                        sub_shift = lax.rem(8 - b8, 8)
                        lane_shift = lax.rem(LANES - rem, LANES)
                        window = slab_ref.at[e, pl.ds(row0, CHUNK_ROWS + 8), pl.ds(lane0, (pieces + 1) * LANES)]
                        tiles = [
                            [window[8 * k:8 * k + 8, LANES * p:LANES * p + LANES] for p in range(pieces + 1)]
                            for k in range(row_vregs + 1)
                        ]
                        out = []
                        for k in range(row_vregs):
                            shifted = [
                                pltpu.roll(jnp.where(sub_mask, tiles[k][p], tiles[k + 1][p]), sub_shift, 0)
                                for p in range(pieces + 1)
                            ]
                            out.append([
                                acc[k][p]
                                + pltpu.roll(jnp.where(lane_mask, shifted[p], shifted[p + 1]), lane_shift, 1)
                                for p in range(pieces)
                            ])
                        return out

                    zero = [[jnp.zeros((8, LANES), jnp.float32) for _ in range(pieces)] for _ in range(row_vregs)]
                    acc = lax.fori_loop(0, epochs, add_epoch, zero, unroll=UNROLL)
                    for k in range(row_vregs):
                        for p in range(pieces):
                            lo = base_o - out_lo + LANES * p
                            out_vmem[img, h, pl.ds(y0 + 8 * k, 8), pl.ds(lo, LANES)] = acc[k][p]
            return carry

        lax.fori_loop(0, hyps, one_hyp, 0)
        for index, out_hbm in enumerate((psi_hbm, phi_hbm)):
            @pl.when(img == index)
            def _():
                copy = pltpu.make_async_copy(
                    out_vmem.at[index, :, :, pl.ds(0, width)],
                    out_hbm.at[:, :, pl.ds(col_base + out_lo, width)],
                    sems.at[index],
                )
                copy.start()
                copy.wait()


def chunk_call(mid, prev, rs, cs, psi_acc, phi_acc, *, index, count, start, rows_out, hyps, cols):
    epochs, images, rows_in, chunk = mid.shape
    side = 2 * LANES
    first = index == 0
    last = index == count - 1
    out_lo = side if first else side - LANES
    out_hi = side + chunk if last else side + chunk - LANES
    col_base = start - side
    kernel = functools.partial(
        chunk_kernel, first=first, last=last, epochs=epochs, hyps=hyps, rows_in=rows_in, rows_out=rows_out,
        chunk=chunk, out_lo=out_lo, out_hi=out_hi, col_base=col_base,
    )
    if psi_acc is None:
        body_kernel = kernel

        def kernel(rs_ref, cs_ref, mid_ref, left_ref, psi_hbm, phi_hbm, *scratch):
            body_kernel(rs_ref, cs_ref, mid_ref, left_ref, None, None, psi_hbm, phi_hbm, *scratch)

    width = out_hi - out_lo
    prev_block = prev.shape[-1] // side - 1
    smem = pltpu.MemorySpace.SMEM
    flops = 2 * epochs * hyps * images * rows_out * width * COST_SCALE
    return pl.pallas_call(
        kernel,
        grid=(images,),
        out_shape=[jax.ShapeDtypeStruct((hyps, rows_out, cols), jnp.float32)] * 2,
        in_specs=[
            pl.BlockSpec(memory_space=smem),
            pl.BlockSpec(memory_space=smem),
            pl.BlockSpec((epochs, 1, rows_in, chunk), lambda i: (0, i, 0, 0)),
            pl.BlockSpec((epochs, 1, rows_in, side), lambda i: (0, i, 0, prev_block)),
        ] + ([] if psi_acc is None else [pl.BlockSpec(memory_space=pl.ANY)] * 2),
        out_specs=[pl.BlockSpec(memory_space=pl.ANY), pl.BlockSpec(memory_space=pl.ANY)],
        scratch_shapes=[
            pltpu.VMEM((epochs, rows_in + 8, side + chunk + LANES), jnp.float32),
            pltpu.VMEM((images, hyps, rows_out, chunk + LANES), jnp.float32),
            pltpu.SemaphoreType.DMA((2,)),
        ],
        input_output_aliases={} if psi_acc is None else {4: 0, 5: 1},
        compiler_params=pltpu.CompilerParams(vmem_limit_bytes=63 * 1024 * 1024),
        cost_estimate=pl.CostEstimate(
            flops=flops, transcendentals=0,
            bytes_accessed=mid.size * 2 + epochs * images * rows_in * side * 2 + 2 * hyps * rows_out * width * 4,
        ),
        name=f"shift_stack_{index}",
    )(rs, cs, mid, prev, *([] if psi_acc is None else [psi_acc, phi_acc]))


def body(psi, phi, row_shift, col_shift):
    row_count = psi.shape[1]
    col_count = psi.shape[2]
    hyp_count = row_shift.shape[1]
    images = jnp.stack([psi, phi], 1)
    extended = with_halo(images, (("sky", 2),), DEPTH)
    bounds = [0] + [b * col_count // SPLIT_BASE for b in SPLIT] + [col_count]
    count = len(bounds) - 1
    pieces = [extended[..., bounds[i]:bounds[i + 1]] for i in range(count)]
    rs = row_shift.reshape(-1)
    cs = col_shift.reshape(-1)
    psi_acc = phi_acc = None
    gathered = [lax.all_gather(pieces[i], "epoch", axis=0, tiled=True) for i in range(min(LOOKAHEAD, count))]
    for i in range(count):
        mid = gathered[i]
        prev = gathered[i - 1] if i > 0 else mid
        psi_acc, phi_acc = chunk_call(
            mid, prev, rs, cs, psi_acc, phi_acc, index=i, count=count, start=bounds[i], rows_out=row_count,
            hyps=hyp_count, cols=col_count,
        )
        ahead = i + LOOKAHEAD
        if ahead < count:
            piece, psi_acc, phi_acc = lax.optimization_barrier((pieces[ahead], psi_acc, phi_acc))
            gathered.append(lax.all_gather(piece, "epoch", axis=0, tiled=True))
    return psi_acc, phi_acc


def solution(mesh):
    return jax.shard_map(
        body,
        mesh=mesh,
        in_specs=(
            P("epoch", "sky", None),
            P("epoch", "sky", None),
            P(None, "epoch"),
            P(None, "epoch"),
        ),
        out_specs=(P("epoch", "sky", None), P("epoch", "sky", None)),
        check_vma=False,
    )
```

```python
import functools

import jax
import jax.numpy as jnp
from jax import lax
from jax.experimental import pallas as pl
from jax.experimental.pallas import tpu as pltpu
from jax.sharding import PartitionSpec as P

DEPTH = 8
XMAX = 64
LANES = 128
BLOCK_COLS = 512
CHUNK_ROWS = 32
SPLIT_BASE = 16
SPLIT = (10,)
COST_SCALE = 1000
LOOKAHEAD = 2
UNROLL = 16


def with_halo(cells, sides, width):
    for axis, dim in sides:
        count = lax.axis_size(axis)
        ends = count - 1
        head = lax.slice_in_dim(cells, 0, width, axis=dim)
        tail = lax.slice_in_dim(cells, cells.shape[dim] - width, cells.shape[dim], axis=dim)
        cells = jnp.concatenate(
            [
                lax.ppermute(tail, axis, [(i, (i + 1) % count) for i in range(ends)]),
                cells,
                lax.ppermute(head, axis, [((i + 1) % count, i) for i in range(ends)]),
            ],
            axis=dim,
        )
    return cells


def chunk_kernel(rs_ref, cs_ref, mid_ref, left_ref, psi_in, phi_in, psi_hbm, phi_hbm, slab_ref, out_vmem, sems,
                 *, first, last, epochs, hyps, rows_in, rows_out, chunk, out_lo, out_hi, col_base):
    side = left_ref.shape[-1]
    slab_rows = slab_ref.shape[1]
    slab_cols = slab_ref.shape[2]
    row_vregs = CHUNK_ROWS // 8
    width = out_hi - out_lo
    subs = []
    at = out_lo
    while at < out_hi:
        pieces = min(BLOCK_COLS // LANES, (out_hi - at) // LANES)
        subs.append((at, pieces))
        at += pieces * LANES
    img = pl.program_id(0)
    if True:
        def convert(e, carry):
            if first:
                slab_ref[e, 0:rows_in, 0:side] = jnp.zeros((rows_in, side), jnp.float32)
            else:
                slab_ref[e, 0:rows_in, 0:side] = left_ref[e, 0].astype(jnp.float32)
            slab_ref[e, 0:rows_in, side:side + chunk] = mid_ref[e, 0].astype(jnp.float32)
            slab_ref[e, 0:rows_in, side + chunk:slab_cols] = jnp.zeros((rows_in, slab_cols - side - chunk), jnp.float32)
            slab_ref[e, rows_in:slab_rows, :] = jnp.zeros((slab_rows - rows_in, slab_cols), jnp.float32)
            return carry

        lax.fori_loop(0, epochs, convert, 0)

        def one_hyp(h, carry):
            for rchunk in range(rows_out // CHUNK_ROWS):
                y0 = rchunk * CHUNK_ROWS
                for base_o, pieces in subs:
                    def add_epoch(e, acc, base_o=base_o, pieces=pieces):
                        start = DEPTH + rs_ref[e * hyps + h]
                        col = cs_ref[e * hyps + h]
                        a8 = start // 8
                        b8 = start - a8 * 8
                        q = (col + LANES) // LANES - 1
                        rem = col - q * LANES
                        row0 = pl.multiple_of(y0 + a8 * 8, 8)
                        lane0 = pl.multiple_of(base_o + q * LANES, LANES)
                        sub_mask = lax.broadcasted_iota(jnp.int32, (8, LANES), 0) >= b8
                        lane_mask = lax.broadcasted_iota(jnp.int32, (8, LANES), 1) >= rem
                        sub_shift = lax.rem(8 - b8, 8)
                        lane_shift = lax.rem(LANES - rem, LANES)
                        window = slab_ref.at[e, pl.ds(row0, CHUNK_ROWS + 8), pl.ds(lane0, (pieces + 1) * LANES)]
                        tiles = [
                            [window[8 * k:8 * k + 8, LANES * p:LANES * p + LANES] for p in range(pieces + 1)]
                            for k in range(row_vregs + 1)
                        ]
                        out = []
                        for k in range(row_vregs):
                            shifted = [
                                pltpu.roll(jnp.where(sub_mask, tiles[k][p], tiles[k + 1][p]), sub_shift, 0)
                                for p in range(pieces + 1)
                            ]
                            out.append([
                                acc[k][p]
                                + pltpu.roll(jnp.where(lane_mask, shifted[p], shifted[p + 1]), lane_shift, 1)
                                for p in range(pieces)
                            ])
                        return out

                    zero = [[jnp.zeros((8, LANES), jnp.float32) for _ in range(pieces)] for _ in range(row_vregs)]
                    acc = lax.fori_loop(0, epochs, add_epoch, zero, unroll=UNROLL)
                    for k in range(row_vregs):
                        for p in range(pieces):
                            lo = base_o - out_lo + LANES * p
                            out_vmem[img, h, pl.ds(y0 + 8 * k, 8), pl.ds(lo, LANES)] = acc[k][p]
            return carry

        lax.fori_loop(0, hyps, one_hyp, 0)
        for index, out_hbm in enumerate((psi_hbm, phi_hbm)):
            @pl.when(img == index)
            def _():
                copy = pltpu.make_async_copy(
                    out_vmem.at[index, :, :, pl.ds(0, width)],
                    out_hbm.at[:, :, pl.ds(col_base + out_lo, width)],
                    sems.at[index],
                )
                copy.start()
                copy.wait()


def chunk_call(mid, prev, rs, cs, psi_acc, phi_acc, *, index, count, start, rows_out, hyps, cols):
    epochs, images, rows_in, chunk = mid.shape
    side = 2 * LANES
    first = index == 0
    last = index == count - 1
    out_lo = side if first else side - LANES
    out_hi = side + chunk if last else side + chunk - LANES
    col_base = start - side
    kernel = functools.partial(
        chunk_kernel, first=first, last=last, epochs=epochs, hyps=hyps, rows_in=rows_in, rows_out=rows_out,
        chunk=chunk, out_lo=out_lo, out_hi=out_hi, col_base=col_base,
    )
    if psi_acc is None:
        body_kernel = kernel

        def kernel(rs_ref, cs_ref, mid_ref, left_ref, psi_hbm, phi_hbm, *scratch):
            body_kernel(rs_ref, cs_ref, mid_ref, left_ref, None, None, psi_hbm, phi_hbm, *scratch)

    width = out_hi - out_lo
    prev_block = prev.shape[-1] // side - 1
    smem = pltpu.MemorySpace.SMEM
    flops = 2 * epochs * hyps * images * rows_out * width * COST_SCALE
    return pl.pallas_call(
        kernel,
        grid=(images,),
        out_shape=[jax.ShapeDtypeStruct((hyps, rows_out, cols), jnp.float32)] * 2,
        in_specs=[
            pl.BlockSpec(memory_space=smem),
            pl.BlockSpec(memory_space=smem),
            pl.BlockSpec((epochs, 1, rows_in, chunk), lambda i: (0, i, 0, 0)),
            pl.BlockSpec((epochs, 1, rows_in, side), lambda i: (0, i, 0, prev_block)),
        ] + ([] if psi_acc is None else [pl.BlockSpec(memory_space=pl.ANY)] * 2),
        out_specs=[pl.BlockSpec(memory_space=pl.ANY), pl.BlockSpec(memory_space=pl.ANY)],
        scratch_shapes=[
            pltpu.VMEM((epochs, rows_in + 8, side + chunk + LANES), jnp.float32),
            pltpu.VMEM((images, hyps, rows_out, chunk + LANES), jnp.float32),
            pltpu.SemaphoreType.DMA((2,)),
        ],
        input_output_aliases={} if psi_acc is None else {4: 0, 5: 1},
        compiler_params=pltpu.CompilerParams(vmem_limit_bytes=63 * 1024 * 1024),
        cost_estimate=pl.CostEstimate(
            flops=flops, transcendentals=0,
            bytes_accessed=mid.size * 2 + epochs * images * rows_in * side * 2 + 2 * hyps * rows_out * width * 4,
        ),
        name=f"shift_stack_{index}",
    )(rs, cs, mid, prev, *([] if psi_acc is None else [psi_acc, phi_acc]))


def body(psi, phi, row_shift, col_shift):
    row_count = psi.shape[1]
    col_count = psi.shape[2]
    hyp_count = row_shift.shape[1]
    images = jnp.stack([psi, phi], 1)
    extended = with_halo(images, (("sky", 2),), DEPTH)
    bounds = [0] + [b * col_count // SPLIT_BASE for b in SPLIT] + [col_count]
    count = len(bounds) - 1
    pieces = [extended[..., bounds[i]:bounds[i + 1]] for i in range(count)]
    rs = row_shift.reshape(-1)
    cs = col_shift.reshape(-1)
    psi_acc = phi_acc = None
    gathered = [lax.all_gather(pieces[i], "epoch", axis=0, tiled=True) for i in range(min(LOOKAHEAD, count))]
    for i in range(count):
        mid = gathered[i]
        prev = gathered[i - 1] if i > 0 else mid
        psi_acc, phi_acc = chunk_call(
            mid, prev, rs, cs, psi_acc, phi_acc, index=i, count=count, start=bounds[i], rows_out=row_count,
            hyps=hyp_count, cols=col_count,
        )
        ahead = i + LOOKAHEAD
        if ahead < count:
            piece, psi_acc, phi_acc = lax.optimization_barrier((pieces[ahead], psi_acc, phi_acc))
            gathered.append(lax.all_gather(piece, "epoch", axis=0, tiled=True))
    return psi_acc, phi_acc


def solution(mesh):
    return jax.shard_map(
        body,
        mesh=mesh,
        in_specs=(
            P("epoch", "sky", None),
            P("epoch", "sky", None),
            P(None, "epoch"),
            P(None, "epoch"),
        ),
        out_specs=(P("epoch", "sky", None), P("epoch", "sky", None)),
        check_vma=False,
    )
```

```python
import functools

import jax
import jax.numpy as jnp
from jax import lax
from jax.experimental import pallas as pl
from jax.experimental.pallas import tpu as pltpu
from jax.sharding import PartitionSpec as P

DEPTH = 8
XMAX = 64
LANES = 128
BLOCK_COLS = 512
CHUNK_ROWS = 32
SPLIT_BASE = 16
SPLIT = (12,)
COST_SCALE = 1000
LOOKAHEAD = 2
UNROLL = 16


def with_halo(cells, sides, width):
    for axis, dim in sides:
        count = lax.axis_size(axis)
        ends = count - 1
        head = lax.slice_in_dim(cells, 0, width, axis=dim)
        tail = lax.slice_in_dim(cells, cells.shape[dim] - width, cells.shape[dim], axis=dim)
        cells = jnp.concatenate(
            [
                lax.ppermute(tail, axis, [(i, (i + 1) % count) for i in range(ends)]),
                cells,
                lax.ppermute(head, axis, [((i + 1) % count, i) for i in range(ends)]),
            ],
            axis=dim,
        )
    return cells


def chunk_kernel(rs_ref, cs_ref, mid_ref, left_ref, psi_in, phi_in, psi_hbm, phi_hbm, slab_ref, out_vmem, sems,
                 *, first, last, epochs, hyps, rows_in, rows_out, chunk, out_lo, out_hi, col_base):
    side = left_ref.shape[-1]
    slab_rows = slab_ref.shape[1]
    slab_cols = slab_ref.shape[2]
    row_vregs = CHUNK_ROWS // 8
    width = out_hi - out_lo
    subs = []
    at = out_lo
    while at < out_hi:
        pieces = min(BLOCK_COLS // LANES, (out_hi - at) // LANES)
        subs.append((at, pieces))
        at += pieces * LANES
    img = pl.program_id(0)
    if True:
        def convert(e, carry):
            if first:
                slab_ref[e, 0:rows_in, 0:side] = jnp.zeros((rows_in, side), jnp.float32)
            else:
                slab_ref[e, 0:rows_in, 0:side] = left_ref[e, 0].astype(jnp.float32)
            slab_ref[e, 0:rows_in, side:side + chunk] = mid_ref[e, 0].astype(jnp.float32)
            slab_ref[e, 0:rows_in, side + chunk:slab_cols] = jnp.zeros((rows_in, slab_cols - side - chunk), jnp.float32)
            slab_ref[e, rows_in:slab_rows, :] = jnp.zeros((slab_rows - rows_in, slab_cols), jnp.float32)
            return carry

        lax.fori_loop(0, epochs, convert, 0)

        def one_hyp(h, carry):
            for rchunk in range(rows_out // CHUNK_ROWS):
                y0 = rchunk * CHUNK_ROWS
                for base_o, pieces in subs:
                    def add_epoch(e, acc, base_o=base_o, pieces=pieces):
                        start = DEPTH + rs_ref[e * hyps + h]
                        col = cs_ref[e * hyps + h]
                        a8 = start // 8
                        b8 = start - a8 * 8
                        q = (col + LANES) // LANES - 1
                        rem = col - q * LANES
                        row0 = pl.multiple_of(y0 + a8 * 8, 8)
                        lane0 = pl.multiple_of(base_o + q * LANES, LANES)
                        sub_mask = lax.broadcasted_iota(jnp.int32, (8, LANES), 0) >= b8
                        lane_mask = lax.broadcasted_iota(jnp.int32, (8, LANES), 1) >= rem
                        sub_shift = lax.rem(8 - b8, 8)
                        lane_shift = lax.rem(LANES - rem, LANES)
                        window = slab_ref.at[e, pl.ds(row0, CHUNK_ROWS + 8), pl.ds(lane0, (pieces + 1) * LANES)]
                        tiles = [
                            [window[8 * k:8 * k + 8, LANES * p:LANES * p + LANES] for p in range(pieces + 1)]
                            for k in range(row_vregs + 1)
                        ]
                        out = []
                        for k in range(row_vregs):
                            shifted = [
                                pltpu.roll(jnp.where(sub_mask, tiles[k][p], tiles[k + 1][p]), sub_shift, 0)
                                for p in range(pieces + 1)
                            ]
                            out.append([
                                acc[k][p]
                                + pltpu.roll(jnp.where(lane_mask, shifted[p], shifted[p + 1]), lane_shift, 1)
                                for p in range(pieces)
                            ])
                        return out

                    zero = [[jnp.zeros((8, LANES), jnp.float32) for _ in range(pieces)] for _ in range(row_vregs)]
                    acc = lax.fori_loop(0, epochs, add_epoch, zero, unroll=UNROLL)
                    for k in range(row_vregs):
                        for p in range(pieces):
                            lo = base_o - out_lo + LANES * p
                            out_vmem[img, h, pl.ds(y0 + 8 * k, 8), pl.ds(lo, LANES)] = acc[k][p]
            return carry

        lax.fori_loop(0, hyps, one_hyp, 0)
        for index, out_hbm in enumerate((psi_hbm, phi_hbm)):
            @pl.when(img == index)
            def _():
                copy = pltpu.make_async_copy(
                    out_vmem.at[index, :, :, pl.ds(0, width)],
                    out_hbm.at[:, :, pl.ds(col_base + out_lo, width)],
                    sems.at[index],
                )
                copy.start()
                copy.wait()


def chunk_call(mid, prev, rs, cs, psi_acc, phi_acc, *, index, count, start, rows_out, hyps, cols):
    epochs, images, rows_in, chunk = mid.shape
    side = 2 * LANES
    first = index == 0
    last = index == count - 1
    out_lo = side if first else side - LANES
    out_hi = side + chunk if last else side + chunk - LANES
    col_base = start - side
    kernel = functools.partial(
        chunk_kernel, first=first, last=last, epochs=epochs, hyps=hyps, rows_in=rows_in, rows_out=rows_out,
        chunk=chunk, out_lo=out_lo, out_hi=out_hi, col_base=col_base,
    )
    if psi_acc is None:
        body_kernel = kernel

        def kernel(rs_ref, cs_ref, mid_ref, left_ref, psi_hbm, phi_hbm, *scratch):
            body_kernel(rs_ref, cs_ref, mid_ref, left_ref, None, None, psi_hbm, phi_hbm, *scratch)

    width = out_hi - out_lo
    prev_block = prev.shape[-1] // side - 1
    smem = pltpu.MemorySpace.SMEM
    flops = 2 * epochs * hyps * images * rows_out * width * COST_SCALE
    return pl.pallas_call(
        kernel,
        grid=(images,),
        out_shape=[jax.ShapeDtypeStruct((hyps, rows_out, cols), jnp.float32)] * 2,
        in_specs=[
            pl.BlockSpec(memory_space=smem),
            pl.BlockSpec(memory_space=smem),
            pl.BlockSpec((epochs, 1, rows_in, chunk), lambda i: (0, i, 0, 0)),
            pl.BlockSpec((epochs, 1, rows_in, side), lambda i: (0, i, 0, prev_block)),
        ] + ([] if psi_acc is None else [pl.BlockSpec(memory_space=pl.ANY)] * 2),
        out_specs=[pl.BlockSpec(memory_space=pl.ANY), pl.BlockSpec(memory_space=pl.ANY)],
        scratch_shapes=[
            pltpu.VMEM((epochs, rows_in + 8, side + chunk + LANES), jnp.float32),
            pltpu.VMEM((images, hyps, rows_out, chunk + LANES), jnp.float32),
            pltpu.SemaphoreType.DMA((2,)),
        ],
        input_output_aliases={} if psi_acc is None else {4: 0, 5: 1},
        compiler_params=pltpu.CompilerParams(vmem_limit_bytes=63 * 1024 * 1024),
        cost_estimate=pl.CostEstimate(
            flops=flops, transcendentals=0,
            bytes_accessed=mid.size * 2 + epochs * images * rows_in * side * 2 + 2 * hyps * rows_out * width * 4,
        ),
        name=f"shift_stack_{index}",
    )(rs, cs, mid, prev, *([] if psi_acc is None else [psi_acc, phi_acc]))


def body(psi, phi, row_shift, col_shift):
    row_count = psi.shape[1]
    col_count = psi.shape[2]
    hyp_count = row_shift.shape[1]
    images = jnp.stack([psi, phi], 1)
    extended = with_halo(images, (("sky", 2),), DEPTH)
    bounds = [0] + [b * col_count // SPLIT_BASE for b in SPLIT] + [col_count]
    count = len(bounds) - 1
    pieces = [extended[..., bounds[i]:bounds[i + 1]] for i in range(count)]
    rs = row_shift.reshape(-1)
    cs = col_shift.reshape(-1)
    psi_acc = phi_acc = None
    gathered = [lax.all_gather(pieces[i], "epoch", axis=0, tiled=True) for i in range(min(LOOKAHEAD, count))]
    for i in range(count):
        mid = gathered[i]
        prev = gathered[i - 1] if i > 0 else mid
        psi_acc, phi_acc = chunk_call(
            mid, prev, rs, cs, psi_acc, phi_acc, index=i, count=count, start=bounds[i], rows_out=row_count,
            hyps=hyp_count, cols=col_count,
        )
        ahead = i + LOOKAHEAD
        if ahead < count:
            piece, psi_acc, phi_acc = lax.optimization_barrier((pieces[ahead], psi_acc, phi_acc))
            gathered.append(lax.all_gather(piece, "epoch", axis=0, tiled=True))
    return psi_acc, phi_acc


def solution(mesh):
    return jax.shard_map(
        body,
        mesh=mesh,
        in_specs=(
            P("epoch", "sky", None),
            P("epoch", "sky", None),
            P(None, "epoch"),
            P(None, "epoch"),
        ),
        out_specs=(P("epoch", "sky", None), P("epoch", "sky", None)),
        check_vma=False,
    )
```

```python
import functools

import jax
import jax.numpy as jnp
from jax import lax
from jax.experimental import pallas as pl
from jax.experimental.pallas import tpu as pltpu
from jax.sharding import PartitionSpec as P

DEPTH = 8
XMAX = 64
LANES = 128
BLOCK_COLS = 640
CHUNK_ROWS = 32
SPLIT_BASE = 16
SPLIT = (12,)
COST_SCALE = 1000
LOOKAHEAD = 2
UNROLL = 16


def with_halo(cells, sides, width):
    for axis, dim in sides:
        count = lax.axis_size(axis)
        ends = count - 1
        head = lax.slice_in_dim(cells, 0, width, axis=dim)
        tail = lax.slice_in_dim(cells, cells.shape[dim] - width, cells.shape[dim], axis=dim)
        cells = jnp.concatenate(
            [
                lax.ppermute(tail, axis, [(i, (i + 1) % count) for i in range(ends)]),
                cells,
                lax.ppermute(head, axis, [((i + 1) % count, i) for i in range(ends)]),
            ],
            axis=dim,
        )
    return cells


def chunk_kernel(rs_ref, cs_ref, mid_ref, left_ref, psi_in, phi_in, psi_hbm, phi_hbm, slab_ref, out_vmem, sems,
                 *, first, last, epochs, hyps, rows_in, rows_out, chunk, out_lo, out_hi, col_base):
    side = left_ref.shape[-1]
    slab_rows = slab_ref.shape[1]
    slab_cols = slab_ref.shape[2]
    row_vregs = CHUNK_ROWS // 8
    width = out_hi - out_lo
    subs = []
    at = out_lo
    while at < out_hi:
        pieces = min(BLOCK_COLS // LANES, (out_hi - at) // LANES)
        subs.append((at, pieces))
        at += pieces * LANES
    img = pl.program_id(0)
    if True:
        def convert(e, carry):
            if first:
                slab_ref[e, 0:rows_in, 0:side] = jnp.zeros((rows_in, side), jnp.float32)
            else:
                slab_ref[e, 0:rows_in, 0:side] = left_ref[e, 0].astype(jnp.float32)
            slab_ref[e, 0:rows_in, side:side + chunk] = mid_ref[e, 0].astype(jnp.float32)
            slab_ref[e, 0:rows_in, side + chunk:slab_cols] = jnp.zeros((rows_in, slab_cols - side - chunk), jnp.float32)
            slab_ref[e, rows_in:slab_rows, :] = jnp.zeros((slab_rows - rows_in, slab_cols), jnp.float32)
            return carry

        lax.fori_loop(0, epochs, convert, 0)

        def one_hyp(h, carry):
            for rchunk in range(rows_out // CHUNK_ROWS):
                y0 = rchunk * CHUNK_ROWS
                for base_o, pieces in subs:
                    def add_epoch(e, acc, base_o=base_o, pieces=pieces):
                        start = DEPTH + rs_ref[e * hyps + h]
                        col = cs_ref[e * hyps + h]
                        a8 = start // 8
                        b8 = start - a8 * 8
                        q = (col + LANES) // LANES - 1
                        rem = col - q * LANES
                        row0 = pl.multiple_of(y0 + a8 * 8, 8)
                        lane0 = pl.multiple_of(base_o + q * LANES, LANES)
                        sub_mask = lax.broadcasted_iota(jnp.int32, (8, LANES), 0) >= b8
                        lane_mask = lax.broadcasted_iota(jnp.int32, (8, LANES), 1) >= rem
                        sub_shift = lax.rem(8 - b8, 8)
                        lane_shift = lax.rem(LANES - rem, LANES)
                        window = slab_ref.at[e, pl.ds(row0, CHUNK_ROWS + 8), pl.ds(lane0, (pieces + 1) * LANES)]
                        tiles = [
                            [window[8 * k:8 * k + 8, LANES * p:LANES * p + LANES] for p in range(pieces + 1)]
                            for k in range(row_vregs + 1)
                        ]
                        out = []
                        for k in range(row_vregs):
                            shifted = [
                                pltpu.roll(jnp.where(sub_mask, tiles[k][p], tiles[k + 1][p]), sub_shift, 0)
                                for p in range(pieces + 1)
                            ]
                            out.append([
                                acc[k][p]
                                + pltpu.roll(jnp.where(lane_mask, shifted[p], shifted[p + 1]), lane_shift, 1)
                                for p in range(pieces)
                            ])
                        return out

                    zero = [[jnp.zeros((8, LANES), jnp.float32) for _ in range(pieces)] for _ in range(row_vregs)]
                    acc = lax.fori_loop(0, epochs, add_epoch, zero, unroll=UNROLL)
                    for k in range(row_vregs):
                        for p in range(pieces):
                            lo = base_o - out_lo + LANES * p
                            out_vmem[img, h, pl.ds(y0 + 8 * k, 8), pl.ds(lo, LANES)] = acc[k][p]
            return carry

        lax.fori_loop(0, hyps, one_hyp, 0)
        for index, out_hbm in enumerate((psi_hbm, phi_hbm)):
            @pl.when(img == index)
            def _():
                copy = pltpu.make_async_copy(
                    out_vmem.at[index, :, :, pl.ds(0, width)],
                    out_hbm.at[:, :, pl.ds(col_base + out_lo, width)],
                    sems.at[index],
                )
                copy.start()
                copy.wait()


def chunk_call(mid, prev, rs, cs, psi_acc, phi_acc, *, index, count, start, rows_out, hyps, cols):
    epochs, images, rows_in, chunk = mid.shape
    side = 2 * LANES
    first = index == 0
    last = index == count - 1
    out_lo = side if first else side - LANES
    out_hi = side + chunk if last else side + chunk - LANES
    col_base = start - side
    kernel = functools.partial(
        chunk_kernel, first=first, last=last, epochs=epochs, hyps=hyps, rows_in=rows_in, rows_out=rows_out,
        chunk=chunk, out_lo=out_lo, out_hi=out_hi, col_base=col_base,
    )
    if psi_acc is None:
        body_kernel = kernel

        def kernel(rs_ref, cs_ref, mid_ref, left_ref, psi_hbm, phi_hbm, *scratch):
            body_kernel(rs_ref, cs_ref, mid_ref, left_ref, None, None, psi_hbm, phi_hbm, *scratch)

    width = out_hi - out_lo
    prev_block = prev.shape[-1] // side - 1
    smem = pltpu.MemorySpace.SMEM
    flops = 2 * epochs * hyps * images * rows_out * width * COST_SCALE
    return pl.pallas_call(
        kernel,
        grid=(images,),
        out_shape=[jax.ShapeDtypeStruct((hyps, rows_out, cols), jnp.float32)] * 2,
        in_specs=[
            pl.BlockSpec(memory_space=smem),
            pl.BlockSpec(memory_space=smem),
            pl.BlockSpec((epochs, 1, rows_in, chunk), lambda i: (0, i, 0, 0)),
            pl.BlockSpec((epochs, 1, rows_in, side), lambda i: (0, i, 0, prev_block)),
        ] + ([] if psi_acc is None else [pl.BlockSpec(memory_space=pl.ANY)] * 2),
        out_specs=[pl.BlockSpec(memory_space=pl.ANY), pl.BlockSpec(memory_space=pl.ANY)],
        scratch_shapes=[
            pltpu.VMEM((epochs, rows_in + 8, side + chunk + LANES), jnp.float32),
            pltpu.VMEM((images, hyps, rows_out, chunk + LANES), jnp.float32),
            pltpu.SemaphoreType.DMA((2,)),
        ],
        input_output_aliases={} if psi_acc is None else {4: 0, 5: 1},
        compiler_params=pltpu.CompilerParams(vmem_limit_bytes=63 * 1024 * 1024),
        cost_estimate=pl.CostEstimate(
            flops=flops, transcendentals=0,
            bytes_accessed=mid.size * 2 + epochs * images * rows_in * side * 2 + 2 * hyps * rows_out * width * 4,
        ),
        name=f"shift_stack_{index}",
    )(rs, cs, mid, prev, *([] if psi_acc is None else [psi_acc, phi_acc]))


def body(psi, phi, row_shift, col_shift):
    row_count = psi.shape[1]
    col_count = psi.shape[2]
    hyp_count = row_shift.shape[1]
    images = jnp.stack([psi, phi], 1)
    extended = with_halo(images, (("sky", 2),), DEPTH)
    bounds = [0] + [b * col_count // SPLIT_BASE for b in SPLIT] + [col_count]
    count = len(bounds) - 1
    pieces = [extended[..., bounds[i]:bounds[i + 1]] for i in range(count)]
    rs = row_shift.reshape(-1)
    cs = col_shift.reshape(-1)
    psi_acc = phi_acc = None
    gathered = [lax.all_gather(pieces[i], "epoch", axis=0, tiled=True) for i in range(min(LOOKAHEAD, count))]
    for i in range(count):
        mid = gathered[i]
        prev = gathered[i - 1] if i > 0 else mid
        psi_acc, phi_acc = chunk_call(
            mid, prev, rs, cs, psi_acc, phi_acc, index=i, count=count, start=bounds[i], rows_out=row_count,
            hyps=hyp_count, cols=col_count,
        )
        ahead = i + LOOKAHEAD
        if ahead < count:
            piece, psi_acc, phi_acc = lax.optimization_barrier((pieces[ahead], psi_acc, phi_acc))
            gathered.append(lax.all_gather(piece, "epoch", axis=0, tiled=True))
    return psi_acc, phi_acc


def solution(mesh):
    return jax.shard_map(
        body,
        mesh=mesh,
        in_specs=(
            P("epoch", "sky", None),
            P("epoch", "sky", None),
            P(None, "epoch"),
            P(None, "epoch"),
        ),
        out_specs=(P("epoch", "sky", None), P("epoch", "sky", None)),
        check_vma=False,
    )
```

```python
import functools

import jax
import jax.numpy as jnp
from jax import lax
from jax.experimental import pallas as pl
from jax.experimental.pallas import tpu as pltpu
from jax.sharding import PartitionSpec as P

DEPTH = 8
XMAX = 64
LANES = 128
BLOCK_COLS = 768
CHUNK_ROWS = 32
SPLIT_BASE = 16
SPLIT = (12,)
COST_SCALE = 1000
LOOKAHEAD = 2
UNROLL = 16


def with_halo(cells, sides, width):
    for axis, dim in sides:
        count = lax.axis_size(axis)
        ends = count - 1
        head = lax.slice_in_dim(cells, 0, width, axis=dim)
        tail = lax.slice_in_dim(cells, cells.shape[dim] - width, cells.shape[dim], axis=dim)
        cells = jnp.concatenate(
            [
                lax.ppermute(tail, axis, [(i, (i + 1) % count) for i in range(ends)]),
                cells,
                lax.ppermute(head, axis, [((i + 1) % count, i) for i in range(ends)]),
            ],
            axis=dim,
        )
    return cells


def chunk_kernel(rs_ref, cs_ref, mid_ref, left_ref, psi_in, phi_in, psi_hbm, phi_hbm, slab_ref, out_vmem, sems,
                 *, first, last, epochs, hyps, rows_in, rows_out, chunk, out_lo, out_hi, col_base):
    side = left_ref.shape[-1]
    slab_rows = slab_ref.shape[1]
    slab_cols = slab_ref.shape[2]
    row_vregs = CHUNK_ROWS // 8
    width = out_hi - out_lo
    subs = []
    at = out_lo
    while at < out_hi:
        pieces = min(BLOCK_COLS // LANES, (out_hi - at) // LANES)
        subs.append((at, pieces))
        at += pieces * LANES
    img = pl.program_id(0)
    if True:
        def convert(e, carry):
            if first:
                slab_ref[e, 0:rows_in, 0:side] = jnp.zeros((rows_in, side), jnp.float32)
            else:
                slab_ref[e, 0:rows_in, 0:side] = left_ref[e, 0].astype(jnp.float32)
            slab_ref[e, 0:rows_in, side:side + chunk] = mid_ref[e, 0].astype(jnp.float32)
            slab_ref[e, 0:rows_in, side + chunk:slab_cols] = jnp.zeros((rows_in, slab_cols - side - chunk), jnp.float32)
            slab_ref[e, rows_in:slab_rows, :] = jnp.zeros((slab_rows - rows_in, slab_cols), jnp.float32)
            return carry

        lax.fori_loop(0, epochs, convert, 0)

        def one_hyp(h, carry):
            for rchunk in range(rows_out // CHUNK_ROWS):
                y0 = rchunk * CHUNK_ROWS
                for base_o, pieces in subs:
                    def add_epoch(e, acc, base_o=base_o, pieces=pieces):
                        start = DEPTH + rs_ref[e * hyps + h]
                        col = cs_ref[e * hyps + h]
                        a8 = start // 8
                        b8 = start - a8 * 8
                        q = (col + LANES) // LANES - 1
                        rem = col - q * LANES
                        row0 = pl.multiple_of(y0 + a8 * 8, 8)
                        lane0 = pl.multiple_of(base_o + q * LANES, LANES)
                        sub_mask = lax.broadcasted_iota(jnp.int32, (8, LANES), 0) >= b8
                        lane_mask = lax.broadcasted_iota(jnp.int32, (8, LANES), 1) >= rem
                        sub_shift = lax.rem(8 - b8, 8)
                        lane_shift = lax.rem(LANES - rem, LANES)
                        window = slab_ref.at[e, pl.ds(row0, CHUNK_ROWS + 8), pl.ds(lane0, (pieces + 1) * LANES)]
                        tiles = [
                            [window[8 * k:8 * k + 8, LANES * p:LANES * p + LANES] for p in range(pieces + 1)]
                            for k in range(row_vregs + 1)
                        ]
                        out = []
                        for k in range(row_vregs):
                            shifted = [
                                pltpu.roll(jnp.where(sub_mask, tiles[k][p], tiles[k + 1][p]), sub_shift, 0)
                                for p in range(pieces + 1)
                            ]
                            out.append([
                                acc[k][p]
                                + pltpu.roll(jnp.where(lane_mask, shifted[p], shifted[p + 1]), lane_shift, 1)
                                for p in range(pieces)
                            ])
                        return out

                    zero = [[jnp.zeros((8, LANES), jnp.float32) for _ in range(pieces)] for _ in range(row_vregs)]
                    acc = lax.fori_loop(0, epochs, add_epoch, zero, unroll=UNROLL)
                    for k in range(row_vregs):
                        for p in range(pieces):
                            lo = base_o - out_lo + LANES * p
                            out_vmem[img, h, pl.ds(y0 + 8 * k, 8), pl.ds(lo, LANES)] = acc[k][p]
            return carry

        lax.fori_loop(0, hyps, one_hyp, 0)
        for index, out_hbm in enumerate((psi_hbm, phi_hbm)):
            @pl.when(img == index)
            def _():
                copy = pltpu.make_async_copy(
                    out_vmem.at[index, :, :, pl.ds(0, width)],
                    out_hbm.at[:, :, pl.ds(col_base + out_lo, width)],
                    sems.at[index],
                )
                copy.start()
                copy.wait()


def chunk_call(mid, prev, rs, cs, psi_acc, phi_acc, *, index, count, start, rows_out, hyps, cols):
    epochs, images, rows_in, chunk = mid.shape
    side = 2 * LANES
    first = index == 0
    last = index == count - 1
    out_lo = side if first else side - LANES
    out_hi = side + chunk if last else side + chunk - LANES
    col_base = start - side
    kernel = functools.partial(
        chunk_kernel, first=first, last=last, epochs=epochs, hyps=hyps, rows_in=rows_in, rows_out=rows_out,
        chunk=chunk, out_lo=out_lo, out_hi=out_hi, col_base=col_base,
    )
    if psi_acc is None:
        body_kernel = kernel

        def kernel(rs_ref, cs_ref, mid_ref, left_ref, psi_hbm, phi_hbm, *scratch):
            body_kernel(rs_ref, cs_ref, mid_ref, left_ref, None, None, psi_hbm, phi_hbm, *scratch)

    width = out_hi - out_lo
    prev_block = prev.shape[-1] // side - 1
    smem = pltpu.MemorySpace.SMEM
    flops = 2 * epochs * hyps * images * rows_out * width * COST_SCALE
    return pl.pallas_call(
        kernel,
        grid=(images,),
        out_shape=[jax.ShapeDtypeStruct((hyps, rows_out, cols), jnp.float32)] * 2,
        in_specs=[
            pl.BlockSpec(memory_space=smem),
            pl.BlockSpec(memory_space=smem),
            pl.BlockSpec((epochs, 1, rows_in, chunk), lambda i: (0, i, 0, 0)),
            pl.BlockSpec((epochs, 1, rows_in, side), lambda i: (0, i, 0, prev_block)),
        ] + ([] if psi_acc is None else [pl.BlockSpec(memory_space=pl.ANY)] * 2),
        out_specs=[pl.BlockSpec(memory_space=pl.ANY), pl.BlockSpec(memory_space=pl.ANY)],
        scratch_shapes=[
            pltpu.VMEM((epochs, rows_in + 8, side + chunk + LANES), jnp.float32),
            pltpu.VMEM((images, hyps, rows_out, chunk + LANES), jnp.float32),
            pltpu.SemaphoreType.DMA((2,)),
        ],
        input_output_aliases={} if psi_acc is None else {4: 0, 5: 1},
        compiler_params=pltpu.CompilerParams(vmem_limit_bytes=63 * 1024 * 1024),
        cost_estimate=pl.CostEstimate(
            flops=flops, transcendentals=0,
            bytes_accessed=mid.size * 2 + epochs * images * rows_in * side * 2 + 2 * hyps * rows_out * width * 4,
        ),
        name=f"shift_stack_{index}",
    )(rs, cs, mid, prev, *([] if psi_acc is None else [psi_acc, phi_acc]))


def body(psi, phi, row_shift, col_shift):
    row_count = psi.shape[1]
    col_count = psi.shape[2]
    hyp_count = row_shift.shape[1]
    images = jnp.stack([psi, phi], 1)
    extended = with_halo(images, (("sky", 2),), DEPTH)
    bounds = [0] + [b * col_count // SPLIT_BASE for b in SPLIT] + [col_count]
    count = len(bounds) - 1
    pieces = [extended[..., bounds[i]:bounds[i + 1]] for i in range(count)]
    rs = row_shift.reshape(-1)
    cs = col_shift.reshape(-1)
    psi_acc = phi_acc = None
    gathered = [lax.all_gather(pieces[i], "epoch", axis=0, tiled=True) for i in range(min(LOOKAHEAD, count))]
    for i in range(count):
        mid = gathered[i]
        prev = gathered[i - 1] if i > 0 else mid
        psi_acc, phi_acc = chunk_call(
            mid, prev, rs, cs, psi_acc, phi_acc, index=i, count=count, start=bounds[i], rows_out=row_count,
            hyps=hyp_count, cols=col_count,
        )
        ahead = i + LOOKAHEAD
        if ahead < count:
            piece, psi_acc, phi_acc = lax.optimization_barrier((pieces[ahead], psi_acc, phi_acc))
            gathered.append(lax.all_gather(piece, "epoch", axis=0, tiled=True))
    return psi_acc, phi_acc


def solution(mesh):
    return jax.shard_map(
        body,
        mesh=mesh,
        in_specs=(
            P("epoch", "sky", None),
            P("epoch", "sky", None),
            P(None, "epoch"),
            P(None, "epoch"),
        ),
        out_specs=(P("epoch", "sky", None), P("epoch", "sky", None)),
        check_vma=False,
    )
```
